256 devices in a mesh: areal: 32 (over x_lo, z, core), layer: 8 (over x_hi, y).
Axes of the slice: x: 4 (x_hi: 2, x_lo: 2; x = x_hi * 2 + x_lo), y: 4, z: 8, core: 2. Of those that a mesh axis runs over, the one named last changes fastest.
Arguments:
- rhs_base: bfloat16 [8, 3, 256, 128, 128], P('layer', None, 'areal'), may hold values from -4 to 4
- perf_rows: bfloat16 [32, 8, 32, 4, 128], P('areal', 'layer'), may hold values from -6 to 6
- perf_cells: int32 [32, 8, 32, 4], P('areal', 'layer'), may hold values from 0 to 1023
- perf_counts: int32 [32, 8, 32], P('areal', 'layer'), may hold values from 0 to 4, as said below
- xface_coef: float32 [8, 3, 256, 128], P('layer', None, 'areal'), may hold values from 0.05 to 0.3
- xface_dir: int32 [8, 3, 256, 128], P('layer', None, 'areal'), may hold values from 0 to 1
- yface_coef: float32 [8, 3, 256, 128], P('layer', None, 'areal'), may hold values from 0.05 to 0.3
- yface_dir: int32 [8, 3, 256, 128], P('layer', None, 'areal'), may hold values from 0 to 1
- cross: float32 [8, 4, 256, 128], P('layer', None, 'areal'), may hold values from -0.6 to 0.6
- newton_count: int32 [4], replicated, may hold values from 2 to 8
- sat_diag: float32 [8, 2, 256, 128], P('layer', None, 'areal'), may hold values from 0.4 to 1
- sat_off: float32 [8, 2, 256, 128], P('layer', None, 'areal'), may hold values from -0.25 to 0.25
- col_diag: float32 [8, 32768], P(None, ('areal', 'layer')), may hold values from 0.3 to 0.6
- col_off: float32 [8, 8, 32768], P(None, None, ('areal', 'layer')), may hold values from -1 to 1
Outputs:
- adjoint: float32 [8, 3, 256, 128, 128], P('layer', None, 'areal')
The draws below stay inside these ranges and needn't reach their ends.
Inputs may be any that keep to these rules, and one draw needn't show every extreme that they name: `perf_cells`: a perforated cell's local index (z * 8 + x) * 128 + y within the receiving tile's slab. `perf_counts`: in every draw one receiving tile gets 4 live slots from every sending tile and slab.
All inputs are finite; a program needn't handle non-finite values.
Results may differ from the reference program's by a relative error of at most 0.0006.
Values may be sent and summed in bfloat16 or wider, within the bound.
No kernel may reach another device: no remote copies, remote signals or barrier semaphores. Data moves between devices by JAX's collectives and lax.ppermute only.
A program may use at most 64 MiB of HBM per device.

```python
import math
import jax
import jax.numpy as jnp
from jax import lax

R = 128
CX = 8
NY = 128
CZ = 1
CAP = 4
ITERS = 4
NEWTON_MAX = 8
STEPS = 4
TILES = 32
SLABS = 8
NX = 256
NZ = 8
COLS = 32768


def draw_perf_counts(key, part):
    base_counts = jax.random.randint(key, (TILES, SLABS, TILES), 0, CAP + 1)
    chosen_tile = jax.random.randint(jax.random.fold_in(key, 11), (), 0, TILES)
    dest_tile = lax.broadcasted_iota(jnp.int32, (TILES, SLABS, TILES), 2)
    return jnp.where(dest_tile == chosen_tile, CAP, base_counts).astype(jnp.int32)


def set_ends(array, rng, low, high):
    extent = array.shape
    index_at = [jax.random.randint(jax.random.fold_in(rng, axis), (), 0, extent[axis]) for axis in range(len(extent))]
    array = array.at[tuple(index_at)].set(low)
    longest = extent.index(max(extent))
    index_at[longest] = (index_at[longest] + 1) % extent[longest]
    return array.at[tuple(index_at)].set(high)


def levels(key, extent, shards, smallest, top_value):
    level, own = 1.0, jax.random.fold_in(key, 6)
    for position, blocks in shards:
        draws = jnp.exp(jax.random.uniform(jax.random.fold_in(own, position), (blocks,), jnp.float32, smallest / len(shards), top_value / len(shards)))
        level = level * jnp.repeat(draws, extent[position] // blocks).reshape([-1 if axis == position else 1 for axis in range(len(extent))])
    return level


def normal_values(key, shape, scale, reach, pieces=(), kind=jnp.bfloat16):
    result = scale * jax.random.normal(key, shape, jnp.float32)
    if pieces:
        result = result * levels(key, shape, pieces, -0.22, 0.18)
    return jnp.clip(result, -reach, reach).astype(kind)


def setup_inputs(seed: int = 0) -> dict:
    splits = jax.random.split(jax.random.key(seed), 15)
    return {
        "rhs_base": normal_values(splits[0], (NZ, 3, NX, NY, R), 1.0, 4.0, ((0, 8), (2, 32))),
        "perf_rows": normal_values(splits[1], (TILES, SLABS, TILES, CAP, R), 1.0, 6.0, ((0, 32), (1, 8))),
        "perf_cells": set_ends(jax.random.randint(splits[2], (TILES, SLABS, TILES, CAP), 0, CZ * CX * NY), jax.random.fold_in(splits[2], 1), 0, (CZ * CX * NY) - 1).astype(jnp.int32),
        "perf_counts": draw_perf_counts(jax.random.fold_in(splits[14], 71), 0),
        "xface_coef": jnp.clip(jnp.exp(math.log(0.3) - 1.7917595 * jax.random.uniform(splits[4], (NZ, 3, NX, NY), jnp.float32) ** levels(splits[4], (NZ, 3, NX, NY), ((0, 8), (2, 32)), -0.2, 0.2)), 0.05, 0.3),
        "xface_dir": set_ends(jax.random.randint(splits[5], (NZ, 3, NX, NY), 0, 2), jax.random.fold_in(splits[5], 1), 0, 1).astype(jnp.int32),
        "yface_coef": jnp.clip(jnp.exp(math.log(0.3) - 1.7917595 * jax.random.uniform(splits[6], (NZ, 3, NX, NY), jnp.float32) ** levels(splits[6], (NZ, 3, NX, NY), ((0, 8), (2, 32)), -0.2, 0.2)), 0.05, 0.3),
        "yface_dir": set_ends(jax.random.randint(splits[7], (NZ, 3, NX, NY), 0, 2), jax.random.fold_in(splits[7], 1), 0, 1).astype(jnp.int32),
        "cross": jnp.clip(jax.random.uniform(splits[8], (NZ, 4, NX, NY), jnp.float32, -0.6, 0.6) * levels(splits[8], (NZ, 4, NX, NY), ((0, 8), (2, 32)), -0.4, 0.0), -0.6, 0.6),
        "newton_count": set_ends(jax.random.randint(splits[9], (STEPS,), 2, NEWTON_MAX + 1), jax.random.fold_in(splits[9], 1), 2, NEWTON_MAX).astype(jnp.int32),
        "sat_diag": jnp.clip(0.4 + 0.6 * jax.random.uniform(splits[10], (NZ, 2, NX, NY), jnp.float32) ** levels(splits[10], (NZ, 2, NX, NY), ((0, 8), (2, 32)), -0.2, 0.2), 0.4, 1.0),
        "sat_off": jnp.clip(jax.random.uniform(splits[11], (NZ, 2, NX, NY), jnp.float32, -0.25, 0.25) * levels(splits[11], (NZ, 2, NX, NY), ((0, 8), (2, 32)), -0.4, 0.0), -0.25, 0.25),
        "col_diag": jnp.clip(0.3 + 0.3 * jax.random.uniform(splits[12], (NZ, COLS), jnp.float32) ** levels(splits[12], (NZ, COLS), ((1, 256),), -0.2, 0.2), 0.3, 0.6),
        "col_off": normal_values(splits[13], (NZ, NZ, COLS), (4 * NZ) ** -0.5, 1.0, ((2, 256),), jnp.float32),
    }


def face_terms(adjoint, coef, direction, axis_dim):
    n_total = adjoint.shape[axis_dim]
    low_side = lax.slice_in_dim(adjoint, 0, n_total - 1, axis=axis_dim)
    high_side = lax.slice_in_dim(adjoint, 1, n_total, axis=axis_dim)
    face_coef = lax.slice_in_dim(coef, 0, n_total - 1, axis=axis_dim)[..., None]
    face_flux = face_coef * (low_side - high_side)
    upwind_far = lax.slice_in_dim(direction, 0, n_total - 1, axis=axis_dim).astype(jnp.float32)[..., None]
    pad_back = [(0, 0)] * adjoint.ndim
    pad_back[axis_dim] = (0, 1)
    pad_front = [(0, 0)] * adjoint.ndim
    pad_front[axis_dim] = (1, 0)
    return jnp.pad((1.0 - upwind_far) * face_flux, pad_back) + jnp.pad(upwind_far * face_flux, pad_front)


def coupling(adjoint, xface_coef, xface_dir, yface_coef, yface_dir, cross, accum_scale):
    upwind = face_terms(adjoint, xface_coef, xface_dir, 2) + face_terms(adjoint, yface_coef, yface_dir, 3)
    mixing = jnp.stack([
        accum_scale * (cross[:, 0, :, :, None] * adjoint[:, 1] + cross[:, 1, :, :, None] * adjoint[:, 2]),
        accum_scale * cross[:, 2, :, :, None] * adjoint[:, 0],
        accum_scale * cross[:, 3, :, :, None] * adjoint[:, 0]], axis=1)
    return upwind + mixing


def reference(rhs_base, perf_rows, perf_cells, perf_counts, xface_coef, xface_dir, yface_coef, yface_dir, cross, newton_count, sat_diag, sat_off, col_diag, col_off):
    slot_live = lax.broadcasted_iota(jnp.int32, perf_cells.shape, 3) < perf_counts[..., None]
    live_rows = jnp.where(slot_live[..., None], perf_rows.astype(jnp.float32), jnp.zeros((), jnp.float32))
    layer_of = lax.broadcasted_iota(jnp.int32, perf_cells.shape, 1)
    tile_of = lax.broadcasted_iota(jnp.int32, perf_cells.shape, 2)
    depth_pos = (layer_of * CZ + perf_cells // (CX * NY)).astype(jnp.int32)
    xpos_cell = (tile_of * CX + (perf_cells // NY) % CX).astype(jnp.int32)
    ypos_cell = (perf_cells % NY).astype(jnp.int32)
    well_source = jnp.zeros((NZ, NX, NY, R), jnp.float32).at[depth_pos, xpos_cell, ypos_cell].add(live_rows)
    source = rhs_base.astype(jnp.float32).at[:, 0].add(well_source)
    accum_scale = jnp.sum(newton_count).astype(jnp.float32) / (STEPS * NEWTON_MAX)
    identity = jnp.eye(NZ, dtype=jnp.float32)
    inverse = col_off + identity[:, :, None] * col_diag[:, None, :]
    adjoint = jnp.zeros_like(source)
    for sweep_index in range(ITERS):
        balance = source - coupling(adjoint, xface_coef, xface_dir, yface_coef, yface_dir, cross, accum_scale)
        pressure_rhs = balance[:, 0].reshape(NZ, NX * NY, R)
        new_press = jnp.einsum("kjc,jcr->kcr", inverse, pressure_rhs, precision=lax.Precision.HIGHEST).reshape(NZ, NX, NY, R)
        sat_one = sat_diag[:, 0, :, :, None] * balance[:, 1] + sat_off[:, 0, :, :, None] * balance[:, 2]
        sat_two = sat_off[:, 1, :, :, None] * balance[:, 1] + sat_diag[:, 1, :, :, None] * balance[:, 2]
        adjoint = jnp.stack([new_press, sat_one, sat_two], axis=1)
    return adjoint
```

```python
import jax
import jax.numpy as jnp
from jax import lax
from jax.sharding import PartitionSpec as P

ITERS = 4
NEWTON_MAX = 8


def passed_along(block, axis, distance):
    devices = range(lax.axis_size(axis))
    route = [(i - distance, i) for i in devices if i - distance in devices]
    return lax.ppermute(block, axis, route)


def x_neighbours(block):
    width_x = block.shape[2]
    low = passed_along(block[:, :, width_x - 1 :].astype(jnp.bfloat16), "areal", 1)
    high = passed_along(block[:, :, :1].astype(jnp.bfloat16), "areal", -1)
    west_vals = jnp.concatenate([low.astype(block.dtype), block[:, :, : width_x - 1]], axis=2)
    east_vals = jnp.concatenate([block[:, :, 1:], high.astype(block.dtype)], axis=2)
    return west_vals, east_vals


def shards(
    rhs_base,
    perf_rows,
    perf_cells,
    perf_counts,
    xface_coef,
    xface_dir,
    yface_coef,
    yface_dir,
    cross,
    newton_count,
    sat_diag,
    sat_off,
    col_diag,
    col_off,
):
    f32 = jnp.float32
    slab_depth, comps, width_x, width_y, rhs_count = rhs_base.shape
    layer_count = lax.axis_size("layer")
    tile_count = lax.axis_size("areal")
    depth = slab_depth * layer_count
    part = rhs_count // layer_count

    rhs_t = jnp.swapaxes(rhs_base, 3, 4).reshape(
        slab_depth, comps, width_x, layer_count, part, width_y
    )
    source = lax.all_to_all(rhs_t, "layer", split_axis=3, concat_axis=0, tiled=True)
    source = source.reshape(depth, comps, width_x, part, width_y).astype(f32)

    send_rows = perf_rows.reshape(perf_rows.shape[2:])
    send_cells = perf_cells.reshape(perf_cells.shape[2:])
    send_counts = perf_counts.reshape(perf_counts.shape[2:])
    slot_live = lax.broadcasted_iota(jnp.int32, send_cells.shape, 1) < send_counts[:, None]
    send_rows = jnp.where(slot_live[:, :, None], send_rows, jnp.zeros_like(send_rows))
    got_rows = lax.all_to_all(send_rows, "areal", split_axis=0, concat_axis=0, tiled=True)
    got_cells = lax.all_to_all(send_cells, "areal", split_axis=0, concat_axis=0, tiled=True)
    slots = got_cells.size
    part_rows = lax.all_to_all(
        got_rows.reshape(1, slots, layer_count, part), "layer", split_axis=2, concat_axis=0, tiled=True
    ).reshape(layer_count, slots, part)
    all_cells = lax.all_gather(got_cells.reshape(1, slots), "layer", axis=0, tiled=True)
    tile_cells = slab_depth * width_x * width_y
    one_hot = (
        lax.broadcasted_iota(jnp.int32, (layer_count, slots, tile_cells), 2) == all_cells[:, :, None]
    ).astype(jnp.bfloat16)
    well = jnp.einsum("lsr,lsc->lrc", part_rows, one_hot, preferred_element_type=f32)
    well = well.reshape(layer_count, part, slab_depth, width_x, width_y)
    well = jnp.transpose(well, (0, 2, 3, 1, 4)).reshape(depth, width_x, part, width_y)
    source = source.at[:, 0].add(well)

    is_last = lax.axis_index("areal") == tile_count - 1
    x_local = lax.broadcasted_iota(jnp.int32, xface_coef.shape, 2)
    east_keep = jnp.where(jnp.logical_and(is_last, x_local == width_x - 1), 0.0, 1.0)
    east_toward = xface_dir.astype(f32)
    east_weight = xface_coef * (1.0 - east_toward) * east_keep
    east_far = xface_coef * east_toward * east_keep
    prev_far = passed_along(east_far[:, :, width_x - 1 :], "areal", 1)
    west_weight = jnp.concatenate([prev_far, east_far[:, :, : width_x - 1]], axis=2)
    y_local = lax.broadcasted_iota(jnp.int32, yface_coef.shape, 3)
    north_keep = jnp.where(y_local == width_y - 1, 0.0, 1.0)
    north_toward = yface_dir.astype(f32)
    north_weight = yface_coef * (1.0 - north_toward) * north_keep
    north_far = yface_coef * north_toward * north_keep
    south_weight = jnp.concatenate(
        [jnp.zeros_like(north_far[:, :, :, :1]), north_far[:, :, :, : width_y - 1]], axis=3
    )
    params = jnp.concatenate(
        [east_weight, west_weight, north_weight, south_weight, cross, sat_diag, sat_off], axis=1
    )
    params = lax.all_gather(params, "layer", axis=0, tiled=True)
    params = params[:, :, :, None, :]
    east_w, west_w, north_w, south_w = (params[:, 3 * i : 3 * i + 3] for i in range(4))
    cr = params[:, 12:16]
    sd = params[:, 16:18]
    so = params[:, 18:20]

    step_count = newton_count.shape[0]
    accum_scale = jnp.sum(newton_count).astype(f32) / (step_count * NEWTON_MAX)

    identity = jnp.eye(col_off.shape[0], dtype=f32)
    inverse = col_off + identity[:, :, None] * col_diag[:, None, :]
    inverse = lax.all_gather(inverse, "layer", axis=2, tiled=True)
    inverse = inverse.reshape(depth, depth, width_x, 1, width_y)

    adjoint = None
    for sweep_index in range(ITERS):
        if sweep_index == 0:
            balance = source
        else:
            west_vals, east_vals = x_neighbours(adjoint)
            zero_row = jnp.zeros_like(adjoint[..., :1])
            north_vals = jnp.concatenate([adjoint[..., 1:], zero_row], axis=4)
            south_vals = jnp.concatenate([zero_row, adjoint[..., :-1]], axis=4)
            upwind = (
                east_w * (adjoint - east_vals)
                + west_w * (west_vals - adjoint)
                + north_w * (adjoint - north_vals)
                + south_w * (south_vals - adjoint)
            )
            mixing = jnp.stack(
                [
                    accum_scale * (cr[:, 0] * adjoint[:, 1] + cr[:, 1] * adjoint[:, 2]),
                    accum_scale * cr[:, 2] * adjoint[:, 0],
                    accum_scale * cr[:, 3] * adjoint[:, 0],
                ],
                axis=1,
            )
            balance = source - (upwind + mixing)
        press_rhs = balance[:, 0]
        new_press = inverse[:, 0] * press_rhs[0][None]
        for j in range(1, depth):
            new_press = new_press + inverse[:, j] * press_rhs[j][None]
        sat_one = sd[:, 0] * balance[:, 1] + so[:, 0] * balance[:, 2]
        sat_two = so[:, 1] * balance[:, 1] + sd[:, 1] * balance[:, 2]
        adjoint = jnp.stack([new_press, sat_one, sat_two], axis=1)

    out = adjoint.reshape(depth, comps, width_x, 1, part, width_y)
    out = lax.all_to_all(out, "layer", split_axis=0, concat_axis=3, tiled=True)
    out = out.reshape(slab_depth, comps, width_x, rhs_count, width_y)
    return jnp.swapaxes(out, 3, 4)


def solution(mesh):
    in_specs = (
        P("layer", None, "areal", None, None),
        P("areal", "layer", None, None, None),
        P("areal", "layer", None, None),
        P("areal", "layer", None),
        P("layer", None, "areal", None),
        P("layer", None, "areal", None),
        P("layer", None, "areal", None),
        P("layer", None, "areal", None),
        P("layer", None, "areal", None),
        P(),
        P("layer", None, "areal", None),
        P("layer", None, "areal", None),
        P(None, ("areal", "layer")),
        P(None, None, ("areal", "layer")),
    )
    out_specs = P("layer", None, "areal", None, None)
    return jax.shard_map(shards, mesh=mesh, in_specs=in_specs, out_specs=out_specs, check_vma=False)
```

```python
import jax
import jax.numpy as jnp
from jax import lax
from jax.sharding import PartitionSpec as P

ITERS = 4
NEWTON_MAX = 8


def passed_along(block, axis, distance):
    devices = range(lax.axis_size(axis))
    route = [(i - distance, i) for i in devices if i - distance in devices]
    return lax.ppermute(block, axis, route)


def x_neighbours(block):
    width_x = block.shape[2]
    low = passed_along(block[:, :, width_x - 1 :].astype(jnp.bfloat16), "areal", 1)
    high = passed_along(block[:, :, :1].astype(jnp.bfloat16), "areal", -1)
    west_vals = jnp.concatenate([low.astype(block.dtype), block[:, :, : width_x - 1]], axis=2)
    east_vals = jnp.concatenate([block[:, :, 1:], high.astype(block.dtype)], axis=2)
    return west_vals, east_vals


def shards(
    rhs_base,
    perf_rows,
    perf_cells,
    perf_counts,
    xface_coef,
    xface_dir,
    yface_coef,
    yface_dir,
    cross,
    newton_count,
    sat_diag,
    sat_off,
    col_diag,
    col_off,
):
    f32 = jnp.float32
    slab_depth, comps, width_x, width_y, rhs_count = rhs_base.shape
    layer_count = lax.axis_size("layer")
    tile_count = lax.axis_size("areal")
    depth = slab_depth * layer_count
    part = rhs_count // layer_count

    rhs_t = jnp.swapaxes(rhs_base, 3, 4).reshape(
        slab_depth, comps, width_x, layer_count, part, width_y
    )
    source = lax.all_to_all(rhs_t, "layer", split_axis=3, concat_axis=0, tiled=True)
    source = source.reshape(depth, comps, width_x, part, width_y).astype(f32)

    is_last = lax.axis_index("areal") == tile_count - 1
    x_local = lax.broadcasted_iota(jnp.int32, xface_coef.shape, 2)
    east_keep = jnp.where(jnp.logical_and(is_last, x_local == width_x - 1), 0.0, 1.0)
    east_toward = xface_dir.astype(f32)
    east_weight = xface_coef * (1.0 - east_toward) * east_keep
    east_far = xface_coef * east_toward * east_keep
    prev_far = passed_along(east_far[:, :, width_x - 1 :], "areal", 1)
    west_weight = jnp.concatenate([prev_far, east_far[:, :, : width_x - 1]], axis=2)
    y_local = lax.broadcasted_iota(jnp.int32, yface_coef.shape, 3)
    north_keep = jnp.where(y_local == width_y - 1, 0.0, 1.0)
    north_toward = yface_dir.astype(f32)
    north_weight = yface_coef * (1.0 - north_toward) * north_keep
    north_far = yface_coef * north_toward * north_keep
    south_weight = jnp.concatenate(
        [jnp.zeros_like(north_far[:, :, :, :1]), north_far[:, :, :, : width_y - 1]], axis=3
    )
    params = jnp.concatenate(
        [east_weight, west_weight, north_weight, south_weight, cross, sat_diag, sat_off], axis=1
    )
    planes = params.shape[1]
    identity = jnp.eye(col_off.shape[0], dtype=f32)
    inverse = col_off + identity[:, :, None] * col_diag[:, None, :]

    send_rows = perf_rows.reshape(perf_rows.shape[2:])
    send_cells = perf_cells.reshape(perf_cells.shape[2:])
    send_counts = perf_counts.reshape(perf_counts.shape[2:])
    cap = send_cells.shape[1]
    slot_live = lax.broadcasted_iota(jnp.int32, send_cells.shape, 1) < send_counts[:, None]
    send_rows = jnp.where(slot_live[:, :, None], send_rows, jnp.zeros_like(send_rows)).astype(f32)
    cell_row = jnp.pad(send_cells.astype(f32), ((0, 0), (0, rhs_count - cap)))[:, None, :]
    got = lax.all_to_all(
        jnp.concatenate([send_rows, cell_row], axis=1), "areal", split_axis=0, concat_axis=0, tiled=True
    )
    slots = got.shape[0] * cap
    got_rows = got[:, :cap, :].reshape(slots, layer_count, part)
    got_cells = got[:, cap, :cap].reshape(slots)

    shared = jnp.concatenate([got_cells, params.reshape(-1), inverse.reshape(-1)])
    payload = jnp.concatenate(
        [
            jnp.transpose(got_rows, (1, 0, 2)).reshape(layer_count, slots * part),
            jnp.broadcast_to(shared[None], (layer_count, shared.shape[0])),
        ],
        axis=1,
    )
    recv = lax.all_to_all(payload, "layer", split_axis=0, concat_axis=0, tiled=True)
    at = slots * part
    part_rows = recv[:, :at].reshape(layer_count, slots, part).astype(jnp.bfloat16)
    all_cells = recv[:, at : at + slots].astype(jnp.int32)
    at += slots
    size = params.size
    params = recv[:, at : at + size].reshape(depth, planes, width_x, width_y)
    at += size
    inverse = recv[:, at:].reshape(layer_count, depth, depth, -1)
    inverse = jnp.transpose(inverse, (1, 2, 0, 3)).reshape(depth, depth, width_x, 1, width_y)

    tile_cells = slab_depth * width_x * width_y
    one_hot = (
        lax.broadcasted_iota(jnp.int32, (layer_count, slots, tile_cells), 2) == all_cells[:, :, None]
    ).astype(jnp.bfloat16)
    well = jnp.einsum("lsr,lsc->lrc", part_rows, one_hot, preferred_element_type=f32)
    well = well.reshape(layer_count, part, slab_depth, width_x, width_y)
    well = jnp.transpose(well, (0, 2, 3, 1, 4)).reshape(depth, width_x, part, width_y)
    source = source.at[:, 0].add(well)

    params = params[:, :, :, None, :]
    east_w, west_w, north_w, south_w = (params[:, 3 * i : 3 * i + 3] for i in range(4))
    cr = params[:, 12:16]
    sd = params[:, 16:18]
    so = params[:, 18:20]

    step_count = newton_count.shape[0]
    accum_scale = jnp.sum(newton_count).astype(f32) / (step_count * NEWTON_MAX)


    adjoint = None
    for sweep_index in range(ITERS):
        if sweep_index == 0:
            balance = source
        else:
            west_vals, east_vals = x_neighbours(adjoint)
            zero_row = jnp.zeros_like(adjoint[..., :1])
            north_vals = jnp.concatenate([adjoint[..., 1:], zero_row], axis=4)
            south_vals = jnp.concatenate([zero_row, adjoint[..., :-1]], axis=4)
            upwind = (
                east_w * (adjoint - east_vals)
                + west_w * (west_vals - adjoint)
                + north_w * (adjoint - north_vals)
                + south_w * (south_vals - adjoint)
            )
            mixing = jnp.stack(
                [
                    accum_scale * (cr[:, 0] * adjoint[:, 1] + cr[:, 1] * adjoint[:, 2]),
                    accum_scale * cr[:, 2] * adjoint[:, 0],
                    accum_scale * cr[:, 3] * adjoint[:, 0],
                ],
                axis=1,
            )
            balance = source - (upwind + mixing)
        press_rhs = balance[:, 0]
        new_press = inverse[:, 0] * press_rhs[0][None]
        for j in range(1, depth):
            new_press = new_press + inverse[:, j] * press_rhs[j][None]
        sat_one = sd[:, 0] * balance[:, 1] + so[:, 0] * balance[:, 2]
        sat_two = so[:, 1] * balance[:, 1] + sd[:, 1] * balance[:, 2]
        adjoint = jnp.stack([new_press, sat_one, sat_two], axis=1)

    out = adjoint.reshape(depth, comps, width_x, 1, part, width_y)
    out = lax.all_to_all(out, "layer", split_axis=0, concat_axis=3, tiled=True)
    out = out.reshape(slab_depth, comps, width_x, rhs_count, width_y)
    return jnp.swapaxes(out, 3, 4)


def solution(mesh):
    in_specs = (
        P("layer", None, "areal", None, None),
        P("areal", "layer", None, None, None),
        P("areal", "layer", None, None),
        P("areal", "layer", None),
        P("layer", None, "areal", None),
        P("layer", None, "areal", None),
        P("layer", None, "areal", None),
        P("layer", None, "areal", None),
        P("layer", None, "areal", None),
        P(),
        P("layer", None, "areal", None),
        P("layer", None, "areal", None),
        P(None, ("areal", "layer")),
        P(None, None, ("areal", "layer")),
    )
    out_specs = P("layer", None, "areal", None, None)
    return jax.shard_map(shards, mesh=mesh, in_specs=in_specs, out_specs=out_specs, check_vma=False)
```

```python
import jax
import jax.numpy as jnp
from jax import lax
from jax.sharding import PartitionSpec as P

ITERS = 4
NEWTON_MAX = 8


def passed_along(block, axis, distance):
    devices = range(lax.axis_size(axis))
    route = [(i - distance, i) for i in devices if i - distance in devices]
    return lax.ppermute(block, axis, route)


def x_neighbours(block):
    width_x = block.shape[2]
    low = passed_along(block[:, :, width_x - 1 :].astype(jnp.bfloat16), "areal", 1)
    high = passed_along(block[:, :, :1].astype(jnp.bfloat16), "areal", -1)
    west_vals = jnp.concatenate([low.astype(block.dtype), block[:, :, : width_x - 1]], axis=2)
    east_vals = jnp.concatenate([block[:, :, 1:], high.astype(block.dtype)], axis=2)
    return west_vals, east_vals


def shards(
    rhs_base,
    perf_rows,
    perf_cells,
    perf_counts,
    xface_coef,
    xface_dir,
    yface_coef,
    yface_dir,
    cross,
    newton_count,
    sat_diag,
    sat_off,
    col_diag,
    col_off,
):
    f32 = jnp.float32
    slab_depth, comps, width_x, width_y, rhs_count = rhs_base.shape
    layer_count = lax.axis_size("layer")
    tile_count = lax.axis_size("areal")
    depth = slab_depth * layer_count
    part = rhs_count // layer_count

    bf16 = jnp.bfloat16

    def split_bf16(values):
        high = lax.reduce_precision(values, exponent_bits=8, mantissa_bits=7)
        return [high.astype(bf16), (values - high).astype(bf16)]

    def join_bf16(high, low):
        return high.astype(f32) + low.astype(f32)

    is_last = lax.axis_index("areal") == tile_count - 1
    x_local = lax.broadcasted_iota(jnp.int32, xface_coef.shape, 2)
    east_keep = jnp.where(jnp.logical_and(is_last, x_local == width_x - 1), 0.0, 1.0)
    x_signed = xface_coef * (1.0 - 2.0 * xface_dir.astype(f32)) * east_keep
    prev_far = passed_along(jnp.maximum(-x_signed[:, :, width_x - 1], 0.0), "areal", 1)
    y_local = lax.broadcasted_iota(jnp.int32, yface_coef.shape, 3)
    north_keep = jnp.where(y_local == width_y - 1, 0.0, 1.0)
    y_signed = yface_coef * (1.0 - 2.0 * yface_dir.astype(f32)) * north_keep
    identity = jnp.eye(col_off.shape[0], dtype=f32)
    inverse = col_off + identity[:, :, None] * col_diag[:, None, :]
    params = jnp.concatenate([x_signed, y_signed, cross, sat_diag, sat_off], axis=1)
    planes = params.shape[1]
    shared = jnp.concatenate([params.reshape(-1), prev_far.reshape(-1), inverse.reshape(-1)])

    send_rows = perf_rows.reshape(perf_rows.shape[2:])
    send_cells = perf_cells.reshape(perf_cells.shape[2:])
    send_counts = perf_counts.reshape(perf_counts.shape[2:])
    cap = send_cells.shape[1]
    slot_live = lax.broadcasted_iota(jnp.int32, send_cells.shape, 1) < send_counts[:, None]
    send_rows = jnp.where(slot_live[:, :, None], send_rows, jnp.zeros_like(send_rows))
    cell_code = jnp.stack([send_cells // 32, send_cells % 32], axis=-1).astype(bf16)

    rhs_t = jnp.swapaxes(rhs_base, 3, 4).reshape(slab_depth, comps, width_x, layer_count, part, width_y)
    rhs_t = jnp.moveaxis(rhs_t, 3, 0).reshape(layer_count, -1)
    rows_t = jnp.moveaxis(send_rows.reshape(tile_count, cap, layer_count, part), 2, 0)
    common = jnp.concatenate([cell_code.reshape(-1)] + split_bf16(shared))
    payload = jnp.concatenate(
        [
            rhs_t,
            rows_t.reshape(layer_count, -1),
            jnp.broadcast_to(common[None], (layer_count, common.shape[0])),
        ],
        axis=1,
    )
    recv = lax.all_to_all(payload, "layer", split_axis=0, concat_axis=0, tiled=True)
    at = rhs_t.shape[1]
    source = recv[:, :at].reshape(depth, comps, width_x, part, width_y).astype(f32)
    size = rows_t[0].size
    slab_rows = recv[:, at : at + size].reshape(layer_count, tile_count, cap, part)
    at += size
    size = cell_code.size
    slab_cells = recv[:, at : at + size].reshape(layer_count, tile_count, cap, 2)
    at += size
    size = shared.shape[0]
    shared = join_bf16(recv[:, at : at + size], recv[:, at + size :])
    size = params.size
    params = shared[:, :size].reshape(depth, planes, width_x, width_y)
    prev_far = shared[:, size : size + comps * width_y].reshape(depth, comps, 1, width_y)
    inverse = shared[:, size + comps * width_y :].reshape(layer_count, depth, depth, -1)
    inverse = jnp.transpose(inverse, (1, 2, 0, 3)).reshape(depth, depth, width_x, 1, width_y)

    areal_send = jnp.concatenate([slab_rows, slab_cells], axis=3)
    areal_send = jnp.moveaxis(areal_send, 1, 0)
    got = lax.all_to_all(areal_send, "areal", split_axis=0, concat_axis=0, tiled=True)
    got = jnp.moveaxis(got, 1, 0).reshape(layer_count, tile_count * cap, part + 2)
    slots = tile_count * cap
    part_rows = got[:, :, :part]
    all_cells = (got[:, :, part].astype(f32) * 32 + got[:, :, part + 1].astype(f32)).astype(jnp.int32)

    tile_cells = slab_depth * width_x * width_y
    one_hot = (
        lax.broadcasted_iota(jnp.int32, (layer_count, slots, tile_cells), 2) == all_cells[:, :, None]
    ).astype(bf16)
    well = jnp.einsum("lsr,lsc->lrc", part_rows, one_hot, preferred_element_type=f32)
    well = well.reshape(layer_count, part, slab_depth, width_x, width_y)
    well = jnp.transpose(well, (0, 2, 3, 1, 4)).reshape(depth, width_x, part, width_y)
    source = source.at[:, 0].add(well)

    x_signed = params[:, 0:3]
    y_signed = params[:, 3:6]
    east_far = jnp.maximum(-x_signed, 0.0)
    north_far = jnp.maximum(-y_signed, 0.0)
    east_w = jnp.maximum(x_signed, 0.0)
    west_w = jnp.concatenate([prev_far, east_far[:, :, : width_x - 1]], axis=2)
    north_w = jnp.maximum(y_signed, 0.0)
    south_w = jnp.concatenate(
        [jnp.zeros_like(north_far[:, :, :, :1]), north_far[:, :, :, : width_y - 1]], axis=3
    )
    east_w, west_w, north_w, south_w = (w[:, :, :, None, :] for w in (east_w, west_w, north_w, south_w))
    params = params[:, :, :, None, :]
    cr = params[:, 6:10]
    sd = params[:, 10:12]
    so = params[:, 12:14]

    step_count = newton_count.shape[0]
    accum_scale = jnp.sum(newton_count).astype(f32) / (step_count * NEWTON_MAX)


    adjoint = None
    for sweep_index in range(ITERS):
        if sweep_index == 0:
            balance = source
        else:
            west_vals, east_vals = x_neighbours(adjoint)
            zero_row = jnp.zeros_like(adjoint[..., :1])
            north_vals = jnp.concatenate([adjoint[..., 1:], zero_row], axis=4)
            south_vals = jnp.concatenate([zero_row, adjoint[..., :-1]], axis=4)
            upwind = (
                east_w * (adjoint - east_vals)
                + west_w * (west_vals - adjoint)
                + north_w * (adjoint - north_vals)
                + south_w * (south_vals - adjoint)
            )
            mixing = jnp.stack(
                [
                    accum_scale * (cr[:, 0] * adjoint[:, 1] + cr[:, 1] * adjoint[:, 2]),
                    accum_scale * cr[:, 2] * adjoint[:, 0],
                    accum_scale * cr[:, 3] * adjoint[:, 0],
                ],
                axis=1,
            )
            balance = source - (upwind + mixing)
        press_rhs = balance[:, 0]
        new_press = inverse[:, 0] * press_rhs[0][None]
        for j in range(1, depth):
            new_press = new_press + inverse[:, j] * press_rhs[j][None]
        sat_one = sd[:, 0] * balance[:, 1] + so[:, 0] * balance[:, 2]
        sat_two = so[:, 1] * balance[:, 1] + sd[:, 1] * balance[:, 2]
        adjoint = jnp.stack([new_press, sat_one, sat_two], axis=1)

    out = adjoint.reshape(depth, comps, width_x, 1, part, width_y)
    out = lax.all_to_all(out, "layer", split_axis=0, concat_axis=3, tiled=True)
    out = out.reshape(slab_depth, comps, width_x, rhs_count, width_y)
    return jnp.swapaxes(out, 3, 4)


def solution(mesh):
    in_specs = (
        P("layer", None, "areal", None, None),
        P("areal", "layer", None, None, None),
        P("areal", "layer", None, None),
        P("areal", "layer", None),
        P("layer", None, "areal", None),
        P("layer", None, "areal", None),
        P("layer", None, "areal", None),
        P("layer", None, "areal", None),
        P("layer", None, "areal", None),
        P(),
        P("layer", None, "areal", None),
        P("layer", None, "areal", None),
        P(None, ("areal", "layer")),
        P(None, None, ("areal", "layer")),
    )
    out_specs = P("layer", None, "areal", None, None)
    return jax.shard_map(shards, mesh=mesh, in_specs=in_specs, out_specs=out_specs, check_vma=False)
```

```python
import jax
import jax.numpy as jnp
from jax import lax
from jax.sharding import PartitionSpec as P

ITERS = 4
NEWTON_MAX = 8


def passed_along(block, axis, distance):
    devices = range(lax.axis_size(axis))
    route = [(i - distance, i) for i in devices if i - distance in devices]
    return lax.ppermute(block, axis, route)


def x_neighbours(block):
    width_x = block.shape[2]
    low = passed_along(block[:, :, width_x - 1 :].astype(jnp.bfloat16), "areal", 1)
    high = passed_along(block[:, :, :1].astype(jnp.bfloat16), "areal", -1)
    west_vals = jnp.concatenate([low.astype(block.dtype), block[:, :, : width_x - 1]], axis=2)
    east_vals = jnp.concatenate([block[:, :, 1:], high.astype(block.dtype)], axis=2)
    return west_vals, east_vals


def shards(
    rhs_base,
    perf_rows,
    perf_cells,
    perf_counts,
    xface_coef,
    xface_dir,
    yface_coef,
    yface_dir,
    cross,
    newton_count,
    sat_diag,
    sat_off,
    col_diag,
    col_off,
):
    f32 = jnp.float32
    slab_depth, comps, width_x, width_y, rhs_count = rhs_base.shape
    layer_count = lax.axis_size("layer")
    tile_count = lax.axis_size("areal")
    depth = slab_depth * layer_count
    part = rhs_count // layer_count

    bf16 = jnp.bfloat16

    def split_bf16(values):
        high = lax.reduce_precision(values, exponent_bits=8, mantissa_bits=7)
        return [high.astype(bf16), (values - high).astype(bf16)]

    def join_bf16(high, low):
        return high.astype(f32) + low.astype(f32)

    is_last = lax.axis_index("areal") == tile_count - 1
    x_local = lax.broadcasted_iota(jnp.int32, xface_coef.shape, 2)
    east_keep = jnp.where(jnp.logical_and(is_last, x_local == width_x - 1), 0.0, 1.0)
    x_signed = xface_coef * (1.0 - 2.0 * xface_dir.astype(f32)) * east_keep
    prev_far = passed_along(jnp.maximum(-x_signed[:, :, width_x - 1], 0.0), "areal", 1)
    y_local = lax.broadcasted_iota(jnp.int32, yface_coef.shape, 3)
    north_keep = jnp.where(y_local == width_y - 1, 0.0, 1.0)
    y_signed = yface_coef * (1.0 - 2.0 * yface_dir.astype(f32)) * north_keep
    identity = jnp.eye(col_off.shape[0], dtype=f32)
    inverse = col_off + identity[:, :, None] * col_diag[:, None, :]
    params = jnp.concatenate([x_signed, y_signed, cross, sat_diag, sat_off], axis=1)
    planes = params.shape[1]

    send_rows = perf_rows.reshape(perf_rows.shape[2:])
    send_cells = perf_cells.reshape(perf_cells.shape[2:])
    send_counts = perf_counts.reshape(perf_counts.shape[2:])
    cap = send_cells.shape[1]
    slot_live = lax.broadcasted_iota(jnp.int32, send_cells.shape, 1) < send_counts[:, None]
    send_rows = jnp.where(slot_live[:, :, None], send_rows, jnp.zeros_like(send_rows))
    cell_code = jnp.concatenate([send_cells // 32, send_cells % 32], axis=1).astype(bf16)
    cell_code = jnp.pad(cell_code, ((0, 0), (0, rhs_count - 2 * cap)))[:, None, :]
    got = lax.all_to_all(
        jnp.concatenate([send_rows, cell_code], axis=1), "areal", split_axis=0, concat_axis=0, tiled=True
    )
    got_rows = got[:, :cap, :]
    got_cells = got[:, cap, :cap].astype(f32) * 32 + got[:, cap, cap : 2 * cap].astype(f32)
    slots = got_cells.size

    lanes = width_y
    rhs_t = jnp.swapaxes(rhs_base, 3, 4).reshape(slab_depth, comps, width_x, layer_count, part, width_y)
    rhs_t = jnp.moveaxis(rhs_t, 3, 0).reshape(layer_count, -1, lanes)
    rows_t = jnp.moveaxis(got_rows.reshape(tile_count, cap, layer_count, part), 2, 0)
    rows_t = rows_t.reshape(layer_count, -1, lanes)
    shared = jnp.concatenate(
        [
            params.reshape(-1, lanes),
            prev_far.reshape(-1, lanes),
            inverse.reshape(-1, lanes),
            got_cells.reshape(-1, lanes),
        ]
    )
    halves = [jnp.broadcast_to(h[None], (layer_count,) + h.shape) for h in split_bf16(shared)]
    payload = jnp.concatenate([rhs_t, rows_t] + halves, axis=1)
    recv = lax.all_to_all(payload, "layer", split_axis=0, concat_axis=0, tiled=True)
    at = rhs_t.shape[1]
    source = recv[:, :at].reshape(depth, comps, width_x, part, width_y).astype(f32)
    size = rows_t.shape[1]
    part_rows = recv[:, at : at + size].reshape(layer_count, slots, part)
    at += size
    size = shared.shape[0]
    shared = join_bf16(recv[:, at : at + size], recv[:, at + size :])
    size = params[0].size // lanes
    params = shared[:, :size].reshape(depth, planes, width_x, width_y)
    prev_far = shared[:, size : size + comps].reshape(depth, comps, 1, width_y)
    at = size + comps
    size = inverse.size // lanes
    inverse = shared[:, at : at + size].reshape(layer_count, depth, depth, -1)
    inverse = jnp.transpose(inverse, (1, 2, 0, 3)).reshape(depth, depth, width_x, 1, width_y)
    all_cells = shared[:, at + size :].reshape(layer_count, slots).astype(jnp.int32)

    tile_cells = slab_depth * width_x * width_y
    one_hot = (
        lax.broadcasted_iota(jnp.int32, (layer_count, slots, tile_cells), 2) == all_cells[:, :, None]
    ).astype(bf16)
    well = jnp.einsum("lsr,lsc->lrc", part_rows, one_hot, preferred_element_type=f32)
    well = well.reshape(layer_count, part, slab_depth, width_x, width_y)
    well = jnp.transpose(well, (0, 2, 3, 1, 4)).reshape(depth, width_x, part, width_y)
    source = source.at[:, 0].add(well)

    x_signed = params[:, 0:3]
    y_signed = params[:, 3:6]
    east_far = jnp.maximum(-x_signed, 0.0)
    north_far = jnp.maximum(-y_signed, 0.0)
    east_w = jnp.maximum(x_signed, 0.0)
    west_w = jnp.concatenate([prev_far, east_far[:, :, : width_x - 1]], axis=2)
    north_w = jnp.maximum(y_signed, 0.0)
    south_w = jnp.concatenate(
        [jnp.zeros_like(north_far[:, :, :, :1]), north_far[:, :, :, : width_y - 1]], axis=3
    )
    east_w, west_w, north_w, south_w = (w[:, :, :, None, :] for w in (east_w, west_w, north_w, south_w))
    params = params[:, :, :, None, :]
    cr = params[:, 6:10]
    sd = params[:, 10:12]
    so = params[:, 12:14]

    step_count = newton_count.shape[0]
    accum_scale = jnp.sum(newton_count).astype(f32) / (step_count * NEWTON_MAX)


    adjoint = None
    for sweep_index in range(ITERS):
        if sweep_index == 0:
            balance = source
        else:
            west_vals, east_vals = x_neighbours(adjoint)
            zero_row = jnp.zeros_like(adjoint[..., :1])
            north_vals = jnp.concatenate([adjoint[..., 1:], zero_row], axis=4)
            south_vals = jnp.concatenate([zero_row, adjoint[..., :-1]], axis=4)
            upwind = (
                east_w * (adjoint - east_vals)
                + west_w * (west_vals - adjoint)
                + north_w * (adjoint - north_vals)
                + south_w * (south_vals - adjoint)
            )
            mixing = jnp.stack(
                [
                    accum_scale * (cr[:, 0] * adjoint[:, 1] + cr[:, 1] * adjoint[:, 2]),
                    accum_scale * cr[:, 2] * adjoint[:, 0],
                    accum_scale * cr[:, 3] * adjoint[:, 0],
                ],
                axis=1,
            )
            balance = source - (upwind + mixing)
        press_rhs = balance[:, 0]
        new_press = inverse[:, 0] * press_rhs[0][None]
        for j in range(1, depth):
            new_press = new_press + inverse[:, j] * press_rhs[j][None]
        sat_one = sd[:, 0] * balance[:, 1] + so[:, 0] * balance[:, 2]
        sat_two = so[:, 1] * balance[:, 1] + sd[:, 1] * balance[:, 2]
        adjoint = jnp.stack([new_press, sat_one, sat_two], axis=1)

    out = adjoint.reshape(depth, comps, width_x, 1, part, width_y)
    out = lax.all_to_all(out, "layer", split_axis=0, concat_axis=3, tiled=True)
    out = out.reshape(slab_depth, comps, width_x, rhs_count, width_y)
    return jnp.swapaxes(out, 3, 4)


def solution(mesh):
    in_specs = (
        P("layer", None, "areal", None, None),
        P("areal", "layer", None, None, None),
        P("areal", "layer", None, None),
        P("areal", "layer", None),
        P("layer", None, "areal", None),
        P("layer", None, "areal", None),
        P("layer", None, "areal", None),
        P("layer", None, "areal", None),
        P("layer", None, "areal", None),
        P(),
        P("layer", None, "areal", None),
        P("layer", None, "areal", None),
        P(None, ("areal", "layer")),
        P(None, None, ("areal", "layer")),
    )
    out_specs = P("layer", None, "areal", None, None)
    return jax.shard_map(shards, mesh=mesh, in_specs=in_specs, out_specs=out_specs, check_vma=False)
```

```python
import jax
import jax.numpy as jnp
from jax import lax
from jax.sharding import PartitionSpec as P

ITERS = 4
NEWTON_MAX = 8


def passed_along(block, axis, distance):
    devices = range(lax.axis_size(axis))
    route = [(i - distance, i) for i in devices if i - distance in devices]
    return lax.ppermute(block, axis, route)


def x_neighbours(block):
    width_x = block.shape[2]
    low = passed_along(block[:, :, width_x - 1 :].astype(jnp.bfloat16), "areal", 1)
    high = passed_along(block[:, :, :1].astype(jnp.bfloat16), "areal", -1)
    west_vals = jnp.concatenate([low.astype(block.dtype), block[:, :, : width_x - 1]], axis=2)
    east_vals = jnp.concatenate([block[:, :, 1:], high.astype(block.dtype)], axis=2)
    return west_vals, east_vals


def shards(
    rhs_base,
    perf_rows,
    perf_cells,
    perf_counts,
    xface_coef,
    xface_dir,
    yface_coef,
    yface_dir,
    cross,
    newton_count,
    sat_diag,
    sat_off,
    col_diag,
    col_off,
):
    f32 = jnp.float32
    slab_depth, comps, width_x, width_y, rhs_count = rhs_base.shape
    layer_count = lax.axis_size("layer")
    tile_count = lax.axis_size("areal")
    depth = slab_depth * layer_count
    part = rhs_count // layer_count

    bf16 = jnp.bfloat16

    def split_bf16(values):
        high = lax.reduce_precision(values, exponent_bits=8, mantissa_bits=7)
        return [high.astype(bf16), (values - high).astype(bf16)]

    def join_bf16(high, low):
        return high.astype(f32) + low.astype(f32)

    is_last = lax.axis_index("areal") == tile_count - 1
    x_local = lax.broadcasted_iota(jnp.int32, xface_coef.shape, 2)
    east_keep = jnp.where(jnp.logical_and(is_last, x_local == width_x - 1), 0.0, 1.0)
    x_signed = xface_coef * (1.0 - 2.0 * xface_dir.astype(f32)) * east_keep
    prev_far = passed_along(jnp.maximum(-x_signed[:, :, width_x - 1], 0.0), "areal", 1)
    y_local = lax.broadcasted_iota(jnp.int32, yface_coef.shape, 3)
    north_keep = jnp.where(y_local == width_y - 1, 0.0, 1.0)
    y_signed = yface_coef * (1.0 - 2.0 * yface_dir.astype(f32)) * north_keep
    identity = jnp.eye(col_off.shape[0], dtype=f32)
    inverse = col_off + identity[:, :, None] * col_diag[:, None, :]
    params = jnp.concatenate([x_signed, y_signed, cross, sat_diag, sat_off], axis=1)
    planes = params.shape[1]

    send_rows = perf_rows.reshape(perf_rows.shape[2:])
    send_cells = perf_cells.reshape(perf_cells.shape[2:])
    send_counts = perf_counts.reshape(perf_counts.shape[2:])
    cap = send_cells.shape[1]
    slot_live = lax.broadcasted_iota(jnp.int32, send_cells.shape, 1) < send_counts[:, None]
    send_rows = jnp.where(slot_live[:, :, None], send_rows, jnp.zeros_like(send_rows))
    cell_code = jnp.concatenate([send_cells // 32, send_cells % 32], axis=1).astype(bf16)
    cell_code = jnp.pad(cell_code, ((0, 0), (0, rhs_count - 2 * cap)))[:, None, :]
    got = lax.all_to_all(
        jnp.concatenate([send_rows, cell_code], axis=1), "areal", split_axis=0, concat_axis=0, tiled=True
    )
    got_rows = got[:, :cap, :]
    got_cells = got[:, cap, :cap].astype(f32) * 32 + got[:, cap, cap : 2 * cap].astype(f32)
    slots = got_cells.size

    lanes = width_y
    rhs_t = jnp.swapaxes(rhs_base, 3, 4).reshape(slab_depth, comps, width_x, layer_count, part, width_y)
    rhs_t = jnp.moveaxis(rhs_t, 3, 0).reshape(layer_count, -1, lanes)
    rows_t = jnp.moveaxis(got_rows.reshape(tile_count, cap, layer_count, part), 2, 0)
    rows_t = rows_t.reshape(layer_count, -1, lanes)
    shared = jnp.concatenate(
        [
            params.reshape(-1, lanes),
            prev_far.reshape(-1, lanes),
            inverse.reshape(-1, lanes),
            got_cells.reshape(-1, lanes),
        ]
    )
    halves = [jnp.broadcast_to(h[None], (layer_count,) + h.shape) for h in split_bf16(shared)]
    payload = jnp.concatenate([rhs_t, rows_t] + halves, axis=1)
    recv = lax.all_to_all(payload, "layer", split_axis=0, concat_axis=0, tiled=True)
    at = rhs_t.shape[1]
    source = recv[:, :at].reshape(depth, comps, width_x, part, width_y).astype(f32)
    size = rows_t.shape[1]
    part_rows = recv[:, at : at + size].reshape(layer_count, slots, part)
    at += size
    size = shared.shape[0]
    shared = join_bf16(recv[:, at : at + size], recv[:, at + size :])
    size = params[0].size // lanes
    params = shared[:, :size].reshape(depth, planes, width_x, width_y)
    prev_far = shared[:, size : size + comps].reshape(depth, comps, 1, width_y)
    at = size + comps
    size = inverse.size // lanes
    inverse = shared[:, at : at + size].reshape(layer_count, depth, depth, -1)
    inverse = jnp.transpose(inverse, (1, 2, 0, 3)).reshape(depth, depth, width_x, 1, width_y)
    all_cells = shared[:, at + size :].reshape(layer_count, slots).astype(jnp.int32)

    tile_cells = slab_depth * width_x * width_y
    one_hot = (
        lax.broadcasted_iota(jnp.int32, (layer_count, slots, tile_cells), 2) == all_cells[:, :, None]
    ).astype(bf16)
    well = jnp.einsum("lsr,lsc->lrc", part_rows, one_hot, preferred_element_type=f32)
    well = well.reshape(layer_count, part, slab_depth, width_x, width_y)
    well = jnp.transpose(well, (0, 2, 3, 1, 4)).reshape(depth, width_x, part, width_y)
    source = source.at[:, 0].add(well)

    x_signed = params[:, 0:3]
    y_signed = params[:, 3:6]
    east_far = jnp.maximum(-x_signed, 0.0)
    north_far = jnp.maximum(-y_signed, 0.0)
    east_w = jnp.maximum(x_signed, 0.0)
    west_w = jnp.concatenate([prev_far, east_far[:, :, : width_x - 1]], axis=2)
    north_w = jnp.maximum(y_signed, 0.0)
    south_w = jnp.concatenate(
        [jnp.zeros_like(north_far[:, :, :, :1]), north_far[:, :, :, : width_y - 1]], axis=3
    )
    east_w, west_w, north_w, south_w = (w[:, :, :, None, :] for w in (east_w, west_w, north_w, south_w))
    params = params[:, :, :, None, :]
    cr = params[:, 6:10]
    sd = params[:, 10:12]
    so = params[:, 12:14]

    step_count = newton_count.shape[0]
    accum_scale = jnp.sum(newton_count).astype(f32) / (step_count * NEWTON_MAX)


    adjoint = None
    for sweep_index in range(ITERS):
        if sweep_index == 0:
            balance = source
        else:
            west_vals, east_vals = x_neighbours(adjoint)
            zero_row = jnp.zeros_like(adjoint[..., :1])
            north_vals = jnp.concatenate([adjoint[..., 1:], zero_row], axis=4)
            south_vals = jnp.concatenate([zero_row, adjoint[..., :-1]], axis=4)
            upwind = (
                east_w * (adjoint - east_vals)
                + west_w * (west_vals - adjoint)
                + north_w * (adjoint - north_vals)
                + south_w * (south_vals - adjoint)
            )
            mixing = jnp.stack(
                [
                    accum_scale * (cr[:, 0] * adjoint[:, 1] + cr[:, 1] * adjoint[:, 2]),
                    accum_scale * cr[:, 2] * adjoint[:, 0],
                    accum_scale * cr[:, 3] * adjoint[:, 0],
                ],
                axis=1,
            )
            balance = source - (upwind + mixing)
        press_rhs = balance[:, 0]
        new_press = inverse[:, 0] * press_rhs[0][None]
        for j in range(1, depth):
            new_press = new_press + inverse[:, j] * press_rhs[j][None]
        sat_one = sd[:, 0] * balance[:, 1] + so[:, 0] * balance[:, 2]
        sat_two = so[:, 1] * balance[:, 1] + sd[:, 1] * balance[:, 2]
        adjoint = jnp.stack([new_press, sat_one, sat_two], axis=1)

    me = lax.axis_index("layer")
    blocks = [lax.dynamic_index_in_dim(adjoint, me, axis=0, keepdims=False)]
    for shift in range(1, layer_count):
        block = lax.dynamic_index_in_dim(adjoint, (me + shift) % layer_count, axis=0, keepdims=False)
        route = [(j, (j + shift) % layer_count) for j in range(layer_count)]
        blocks.append(lax.ppermute(block, "layer", route))
    order = (me - jnp.arange(layer_count)) % layer_count
    out = jnp.take(jnp.stack(blocks), order, axis=0)
    out = jnp.moveaxis(out, 0, 2).reshape(slab_depth, comps, width_x, rhs_count, width_y)
    return jnp.swapaxes(out, 3, 4)


def solution(mesh):
    in_specs = (
        P("layer", None, "areal", None, None),
        P("areal", "layer", None, None, None),
        P("areal", "layer", None, None),
        P("areal", "layer", None),
        P("layer", None, "areal", None),
        P("layer", None, "areal", None),
        P("layer", None, "areal", None),
        P("layer", None, "areal", None),
        P("layer", None, "areal", None),
        P(),
        P("layer", None, "areal", None),
        P("layer", None, "areal", None),
        P(None, ("areal", "layer")),
        P(None, None, ("areal", "layer")),
    )
    out_specs = P("layer", None, "areal", None, None)
    return jax.shard_map(shards, mesh=mesh, in_specs=in_specs, out_specs=out_specs, check_vma=False)
```

```python
import jax
import jax.numpy as jnp
from jax import lax
from jax.sharding import PartitionSpec as P

ITERS = 4
NEWTON_MAX = 8


def passed_along(block, axis, distance):
    devices = range(lax.axis_size(axis))
    route = [(i - distance, i) for i in devices if i - distance in devices]
    return lax.ppermute(block, axis, route)


def x_neighbours(block):
    width_x = block.shape[2]
    low = passed_along(block[:, :, width_x - 1 :].astype(jnp.bfloat16), "areal", 1)
    high = passed_along(block[:, :, :1].astype(jnp.bfloat16), "areal", -1)
    west_vals = jnp.concatenate([low.astype(block.dtype), block[:, :, : width_x - 1]], axis=2)
    east_vals = jnp.concatenate([block[:, :, 1:], high.astype(block.dtype)], axis=2)
    return west_vals, east_vals


def shards(
    rhs_base,
    perf_rows,
    perf_cells,
    perf_counts,
    xface_coef,
    xface_dir,
    yface_coef,
    yface_dir,
    cross,
    newton_count,
    sat_diag,
    sat_off,
    col_diag,
    col_off,
):
    f32 = jnp.float32
    slab_depth, comps, width_x, width_y, rhs_count = rhs_base.shape
    layer_count = lax.axis_size("layer")
    tile_count = lax.axis_size("areal")
    depth = slab_depth * layer_count
    part = rhs_count // layer_count

    bf16 = jnp.bfloat16

    def split_bf16(values):
        high = lax.reduce_precision(values, exponent_bits=8, mantissa_bits=7)
        return [high.astype(bf16), (values - high).astype(bf16)]

    def join_bf16(high, low):
        return high.astype(f32) + low.astype(f32)

    is_last = lax.axis_index("areal") == tile_count - 1
    x_local = lax.broadcasted_iota(jnp.int32, xface_coef.shape, 2)
    east_keep = jnp.where(jnp.logical_and(is_last, x_local == width_x - 1), 0.0, 1.0)
    x_signed = xface_coef * (1.0 - 2.0 * xface_dir.astype(f32)) * east_keep
    prev_far = passed_along(jnp.maximum(-x_signed[:, :, width_x - 1], 0.0), "areal", 1)
    y_local = lax.broadcasted_iota(jnp.int32, yface_coef.shape, 3)
    north_keep = jnp.where(y_local == width_y - 1, 0.0, 1.0)
    y_signed = yface_coef * (1.0 - 2.0 * yface_dir.astype(f32)) * north_keep
    identity = jnp.eye(col_off.shape[0], dtype=f32)
    inverse = col_off + identity[:, :, None] * col_diag[:, None, :]
    params = jnp.concatenate([x_signed, y_signed, cross, sat_diag, sat_off], axis=1)
    planes = params.shape[1]

    send_rows = perf_rows.reshape(perf_rows.shape[2:])
    send_cells = perf_cells.reshape(perf_cells.shape[2:])
    send_counts = perf_counts.reshape(perf_counts.shape[2:])
    cap = send_cells.shape[1]
    slot_live = lax.broadcasted_iota(jnp.int32, send_cells.shape, 1) < send_counts[:, None]
    send_rows = jnp.where(slot_live[:, :, None], send_rows, jnp.zeros_like(send_rows))
    cell_code = jnp.concatenate([send_cells // 32, send_cells % 32], axis=1).astype(bf16)
    cell_code = jnp.pad(cell_code, ((0, 0), (0, rhs_count - 2 * cap)))[:, None, :]
    got = lax.all_to_all(
        jnp.concatenate([send_rows, cell_code], axis=1), "areal", split_axis=0, concat_axis=0, tiled=True
    )
    got_rows = got[:, :cap, :]
    got_cells = got[:, cap, :cap].astype(f32) * 32 + got[:, cap, cap : 2 * cap].astype(f32)
    slots = got_cells.size

    lanes = width_y
    rhs_t = jnp.swapaxes(rhs_base, 3, 4).reshape(slab_depth, comps, width_x, layer_count, part, width_y)
    rhs_t = jnp.moveaxis(rhs_t, 3, 0).reshape(layer_count, -1, lanes)
    rows_t = jnp.moveaxis(got_rows.reshape(tile_count, cap, layer_count, part), 2, 0)
    rows_t = rows_t.reshape(layer_count, -1, lanes)
    shared = jnp.concatenate(
        [
            params.reshape(-1, lanes),
            prev_far.reshape(-1, lanes),
            inverse.reshape(-1, lanes),
            got_cells.reshape(-1, lanes),
        ]
    )
    halves = [jnp.broadcast_to(h[None], (layer_count,) + h.shape) for h in split_bf16(shared)]
    payload = jnp.concatenate([rhs_t, rows_t] + halves, axis=1)
    recv = lax.all_to_all(payload, "layer", split_axis=0, concat_axis=0, tiled=True)
    at = rhs_t.shape[1]
    source = recv[:, :at].reshape(depth, comps, width_x, part, width_y).astype(f32)
    size = rows_t.shape[1]
    part_rows = recv[:, at : at + size].reshape(layer_count, slots, part)
    at += size
    size = shared.shape[0]
    shared = join_bf16(recv[:, at : at + size], recv[:, at + size :])
    size = params[0].size // lanes
    params = shared[:, :size].reshape(depth, planes, width_x, width_y)
    prev_far = shared[:, size : size + comps].reshape(depth, comps, 1, width_y)
    at = size + comps
    size = inverse.size // lanes
    inverse = shared[:, at : at + size].reshape(layer_count, depth, depth, -1)
    inverse = jnp.transpose(inverse, (1, 2, 0, 3)).reshape(depth, depth, width_x, 1, width_y)
    all_cells = shared[:, at + size :].reshape(layer_count, slots).astype(jnp.int32)

    tile_cells = slab_depth * width_x * width_y
    one_hot = (
        lax.broadcasted_iota(jnp.int32, (layer_count, slots, tile_cells), 2) == all_cells[:, :, None]
    ).astype(bf16)
    well = jnp.einsum("lsr,lsc->lrc", part_rows, one_hot, preferred_element_type=f32)
    well = well.reshape(layer_count, part, slab_depth, width_x, width_y)
    well = jnp.transpose(well, (0, 2, 3, 1, 4)).reshape(depth, width_x, part, width_y)
    source = source.at[:, 0].add(well)

    x_signed = params[:, 0:3]
    y_signed = params[:, 3:6]
    east_far = jnp.maximum(-x_signed, 0.0)
    north_far = jnp.maximum(-y_signed, 0.0)
    east_w = jnp.maximum(x_signed, 0.0)
    west_w = jnp.concatenate([prev_far, east_far[:, :, : width_x - 1]], axis=2)
    north_w = jnp.maximum(y_signed, 0.0)
    south_w = jnp.concatenate(
        [jnp.zeros_like(north_far[:, :, :, :1]), north_far[:, :, :, : width_y - 1]], axis=3
    )
    east_w, west_w, north_w, south_w = (w[:, :, :, None, :] for w in (east_w, west_w, north_w, south_w))
    params = params[:, :, :, None, :]
    cr = params[:, 6:10]
    sd = params[:, 10:12]
    so = params[:, 12:14]

    step_count = newton_count.shape[0]
    accum_scale = jnp.sum(newton_count).astype(f32) / (step_count * NEWTON_MAX)


    def solve(balance, inv, diag, off):
        press_rhs = balance[:, 0]
        new_press = inv[:, 0] * press_rhs[0][None]
        for j in range(1, depth):
            new_press = new_press + inv[:, j] * press_rhs[j][None]
        sat_one = diag[:, 0] * balance[:, 1] + off[:, 0] * balance[:, 2]
        sat_two = off[:, 1] * balance[:, 1] + diag[:, 1] * balance[:, 2]
        return jnp.stack([new_press, sat_one, sat_two], axis=1)

    def sweep_rows(center, west_vals, east_vals, data):
        src, ew, ww, nw, sw, c, dg, of, inv = data
        zero_row = jnp.zeros_like(center[..., :1])
        north_vals = jnp.concatenate([center[..., 1:], zero_row], axis=4)
        south_vals = jnp.concatenate([zero_row, center[..., :-1]], axis=4)
        upwind = (
            ew * (center - east_vals)
            + ww * (west_vals - center)
            + nw * (center - north_vals)
            + sw * (south_vals - center)
        )
        mixing = jnp.stack(
            [
                accum_scale * (c[:, 0] * center[:, 1] + c[:, 1] * center[:, 2]),
                accum_scale * c[:, 2] * center[:, 0],
                accum_scale * c[:, 3] * center[:, 0],
            ],
            axis=1,
        )
        return solve(src - (upwind + mixing), inv, dg, of)

    def sweep_tile(adjoint, west_row, east_row, data):
        west_vals = jnp.concatenate([west_row, adjoint[:, :, : width_x - 1]], axis=2)
        east_vals = jnp.concatenate([adjoint[:, :, 1:], east_row], axis=2)
        return sweep_rows(adjoint, west_vals, east_vals, data)

    data = (source, east_w, west_w, north_w, south_w, cr, sd, so, inverse)

    def row_pack(row):
        return jnp.concatenate([d[:, :, row : row + 1].reshape(-1, width_y) for d in data])

    def row_unpack(pack):
        fields, at = [], 0
        for d in data:
            shape = d[:, :, :1].shape
            size = d[:, :, :1].size // width_y
            fields.append(pack[at : at + size].reshape(shape))
            at += size
        return tuple(fields)

    west_data = row_unpack(passed_along(row_pack(width_x - 1), "areal", 1))
    east_data = row_unpack(passed_along(row_pack(0), "areal", -1))

    def halo(block, rows):
        low = passed_along(block[:, :, width_x - rows :].astype(bf16), "areal", 1).astype(f32)
        high = passed_along(block[:, :, :rows].astype(bf16), "areal", -1).astype(f32)
        return low, high

    adjoint = solve(source, inverse, sd, so)
    low, high = halo(adjoint, 2)
    west_edge = sweep_rows(low[:, :, 1:], low[:, :, :1], adjoint[:, :, :1], west_data)
    east_edge = sweep_rows(high[:, :, :1], adjoint[:, :, width_x - 1 :], high[:, :, 1:], east_data)
    adjoint = sweep_tile(adjoint, low[:, :, 1:], high[:, :, :1], data)
    adjoint = sweep_tile(adjoint, west_edge, east_edge, data)
    for sweep_index in range(3, ITERS):
        low, high = halo(adjoint, 1)
        adjoint = sweep_tile(adjoint, low, high, data)

    out = adjoint.reshape(depth, comps, width_x, 1, part, width_y)
    out = lax.all_to_all(out, "layer", split_axis=0, concat_axis=3, tiled=True)
    out = out.reshape(slab_depth, comps, width_x, rhs_count, width_y)
    return jnp.swapaxes(out, 3, 4)


def solution(mesh):
    in_specs = (
        P("layer", None, "areal", None, None),
        P("areal", "layer", None, None, None),
        P("areal", "layer", None, None),
        P("areal", "layer", None),
        P("layer", None, "areal", None),
        P("layer", None, "areal", None),
        P("layer", None, "areal", None),
        P("layer", None, "areal", None),
        P("layer", None, "areal", None),
        P(),
        P("layer", None, "areal", None),
        P("layer", None, "areal", None),
        P(None, ("areal", "layer")),
        P(None, None, ("areal", "layer")),
    )
    out_specs = P("layer", None, "areal", None, None)
    return jax.shard_map(shards, mesh=mesh, in_specs=in_specs, out_specs=out_specs, check_vma=False)
```

```python
import jax
import jax.numpy as jnp
from jax import lax
from jax.sharding import PartitionSpec as P

ITERS = 4
NEWTON_MAX = 8


def passed_along(block, axis, distance):
    devices = range(lax.axis_size(axis))
    route = [(i - distance, i) for i in devices if i - distance in devices]
    return lax.ppermute(block, axis, route)


def x_neighbours(block):
    width_x = block.shape[2]
    low = passed_along(block[:, :, width_x - 1 :].astype(jnp.bfloat16), "areal", 1)
    high = passed_along(block[:, :, :1].astype(jnp.bfloat16), "areal", -1)
    west_vals = jnp.concatenate([low.astype(block.dtype), block[:, :, : width_x - 1]], axis=2)
    east_vals = jnp.concatenate([block[:, :, 1:], high.astype(block.dtype)], axis=2)
    return west_vals, east_vals


def shards(
    rhs_base,
    perf_rows,
    perf_cells,
    perf_counts,
    xface_coef,
    xface_dir,
    yface_coef,
    yface_dir,
    cross,
    newton_count,
    sat_diag,
    sat_off,
    col_diag,
    col_off,
):
    f32 = jnp.float32
    slab_depth, comps, width_x, width_y, rhs_count = rhs_base.shape
    layer_count = lax.axis_size("layer")
    tile_count = lax.axis_size("areal")
    depth = slab_depth * layer_count
    part = rhs_count // layer_count

    bf16 = jnp.bfloat16

    def split_bf16(values):
        high = lax.reduce_precision(values, exponent_bits=8, mantissa_bits=7)
        return [high.astype(bf16), (values - high).astype(bf16)]

    def join_bf16(high, low):
        return high.astype(f32) + low.astype(f32)

    is_last = lax.axis_index("areal") == tile_count - 1
    x_local = lax.broadcasted_iota(jnp.int32, xface_coef.shape, 2)
    east_keep = jnp.where(jnp.logical_and(is_last, x_local == width_x - 1), 0.0, 1.0)
    x_signed = xface_coef * (1.0 - 2.0 * xface_dir.astype(f32)) * east_keep
    prev_far = passed_along(jnp.maximum(-x_signed[:, :, width_x - 1], 0.0), "areal", 1)
    y_local = lax.broadcasted_iota(jnp.int32, yface_coef.shape, 3)
    north_keep = jnp.where(y_local == width_y - 1, 0.0, 1.0)
    y_signed = yface_coef * (1.0 - 2.0 * yface_dir.astype(f32)) * north_keep
    identity = jnp.eye(col_off.shape[0], dtype=f32)
    inverse = col_off + identity[:, :, None] * col_diag[:, None, :]
    params = jnp.concatenate([x_signed, y_signed, cross, sat_diag, sat_off], axis=1)
    planes = params.shape[1]

    send_rows = perf_rows.reshape(perf_rows.shape[2:])
    send_cells = perf_cells.reshape(perf_cells.shape[2:])
    send_counts = perf_counts.reshape(perf_counts.shape[2:])
    cap = send_cells.shape[1]
    slot_live = lax.broadcasted_iota(jnp.int32, send_cells.shape, 1) < send_counts[:, None]
    send_rows = jnp.where(slot_live[:, :, None], send_rows, jnp.zeros_like(send_rows))
    cell_code = jnp.concatenate([send_cells // 32, send_cells % 32], axis=1).astype(bf16)
    cell_code = jnp.pad(cell_code, ((0, 0), (0, rhs_count - 2 * cap)))[:, None, :]
    got = lax.all_to_all(
        jnp.concatenate([send_rows, cell_code], axis=1), "areal", split_axis=0, concat_axis=0, tiled=True
    )
    got_rows = got[:, :cap, :]
    slots = tile_count * cap

    lanes = width_y
    shared = jnp.concatenate(
        [params.reshape(-1, lanes), prev_far.reshape(-1, lanes), inverse.reshape(-1, lanes)]
    )
    me = lax.axis_index("layer")
    blocks = [shared]
    for shift in range(1, layer_count):
        route = [(j, (j + shift) % layer_count) for j in range(layer_count)]
        blocks.append(lax.ppermute(shared, "layer", route))
    order = (me - jnp.arange(layer_count)) % layer_count
    shared = jnp.take(jnp.stack(blocks), order, axis=0)

    rhs_t = jnp.swapaxes(rhs_base, 3, 4).reshape(slab_depth, comps, width_x, layer_count, part, width_y)
    rhs_t = jnp.moveaxis(rhs_t, 3, 0).reshape(layer_count, -1, lanes)
    rows_t = jnp.moveaxis(got_rows.reshape(tile_count, cap, layer_count, part), 2, 0)
    rows_t = rows_t.reshape(layer_count, -1, lanes)
    cell_rows = jnp.stack([got[:, cap, :cap], got[:, cap, cap : 2 * cap]]).reshape(2, lanes)
    cell_rows = jnp.broadcast_to(cell_rows[None], (layer_count, 2, lanes))
    payload = jnp.concatenate([rhs_t, rows_t, cell_rows], axis=1)
    recv = lax.all_to_all(payload, "layer", split_axis=0, concat_axis=0, tiled=True)
    at = rhs_t.shape[1]
    source = recv[:, :at].reshape(depth, comps, width_x, part, width_y).astype(f32)
    size = rows_t.shape[1]
    part_rows = recv[:, at : at + size].reshape(layer_count, slots, part)
    at += size
    all_cells = recv[:, at].astype(f32) * 32 + recv[:, at + 1].astype(f32)
    all_cells = all_cells.astype(jnp.int32)
    size = params[0].size // lanes
    params = shared[:, :size].reshape(depth, planes, width_x, width_y)
    prev_far = shared[:, size : size + comps].reshape(depth, comps, 1, width_y)
    at = size + comps
    inverse = shared[:, at:].reshape(layer_count, depth, depth, -1)
    inverse = jnp.transpose(inverse, (1, 2, 0, 3)).reshape(depth, depth, width_x, 1, width_y)

    tile_cells = slab_depth * width_x * width_y
    one_hot = (
        lax.broadcasted_iota(jnp.int32, (layer_count, slots, tile_cells), 2) == all_cells[:, :, None]
    ).astype(bf16)
    well = jnp.einsum("lsr,lsc->lrc", part_rows, one_hot, preferred_element_type=f32)
    well = well.reshape(layer_count, part, slab_depth, width_x, width_y)
    well = jnp.transpose(well, (0, 2, 3, 1, 4)).reshape(depth, width_x, part, width_y)
    source = source.at[:, 0].add(well)

    x_signed = params[:, 0:3]
    y_signed = params[:, 3:6]
    east_far = jnp.maximum(-x_signed, 0.0)
    north_far = jnp.maximum(-y_signed, 0.0)
    east_w = jnp.maximum(x_signed, 0.0)
    west_w = jnp.concatenate([prev_far, east_far[:, :, : width_x - 1]], axis=2)
    north_w = jnp.maximum(y_signed, 0.0)
    south_w = jnp.concatenate(
        [jnp.zeros_like(north_far[:, :, :, :1]), north_far[:, :, :, : width_y - 1]], axis=3
    )
    east_w, west_w, north_w, south_w = (w[:, :, :, None, :] for w in (east_w, west_w, north_w, south_w))
    params = params[:, :, :, None, :]
    cr = params[:, 6:10]
    sd = params[:, 10:12]
    so = params[:, 12:14]

    step_count = newton_count.shape[0]
    accum_scale = jnp.sum(newton_count).astype(f32) / (step_count * NEWTON_MAX)


    adjoint = None
    for sweep_index in range(ITERS):
        if sweep_index == 0:
            balance = source
        else:
            west_vals, east_vals = x_neighbours(adjoint)
            zero_row = jnp.zeros_like(adjoint[..., :1])
            north_vals = jnp.concatenate([adjoint[..., 1:], zero_row], axis=4)
            south_vals = jnp.concatenate([zero_row, adjoint[..., :-1]], axis=4)
            upwind = (
                east_w * (adjoint - east_vals)
                + west_w * (west_vals - adjoint)
                + north_w * (adjoint - north_vals)
                + south_w * (south_vals - adjoint)
            )
            mixing = jnp.stack(
                [
                    accum_scale * (cr[:, 0] * adjoint[:, 1] + cr[:, 1] * adjoint[:, 2]),
                    accum_scale * cr[:, 2] * adjoint[:, 0],
                    accum_scale * cr[:, 3] * adjoint[:, 0],
                ],
                axis=1,
            )
            balance = source - (upwind + mixing)
        press_rhs = balance[:, 0]
        new_press = inverse[:, 0] * press_rhs[0][None]
        for j in range(1, depth):
            new_press = new_press + inverse[:, j] * press_rhs[j][None]
        sat_one = sd[:, 0] * balance[:, 1] + so[:, 0] * balance[:, 2]
        sat_two = so[:, 1] * balance[:, 1] + sd[:, 1] * balance[:, 2]
        adjoint = jnp.stack([new_press, sat_one, sat_two], axis=1)

    out = adjoint.reshape(depth, comps, width_x, 1, part, width_y)
    out = lax.all_to_all(out, "layer", split_axis=0, concat_axis=3, tiled=True)
    out = out.reshape(slab_depth, comps, width_x, rhs_count, width_y)
    return jnp.swapaxes(out, 3, 4)


def solution(mesh):
    in_specs = (
        P("layer", None, "areal", None, None),
        P("areal", "layer", None, None, None),
        P("areal", "layer", None, None),
        P("areal", "layer", None),
        P("layer", None, "areal", None),
        P("layer", None, "areal", None),
        P("layer", None, "areal", None),
        P("layer", None, "areal", None),
        P("layer", None, "areal", None),
        P(),
        P("layer", None, "areal", None),
        P("layer", None, "areal", None),
        P(None, ("areal", "layer")),
        P(None, None, ("areal", "layer")),
    )
    out_specs = P("layer", None, "areal", None, None)
    return jax.shard_map(shards, mesh=mesh, in_specs=in_specs, out_specs=out_specs, check_vma=False)
```

```python
import jax
import jax.numpy as jnp
from jax import lax
from jax.sharding import PartitionSpec as P

ITERS = 4
NEWTON_MAX = 8


def passed_along(block, axis, distance):
    devices = range(lax.axis_size(axis))
    route = [(i - distance, i) for i in devices if i - distance in devices]
    return lax.ppermute(block, axis, route)


def x_neighbours(block):
    width_x = block.shape[2]
    low = passed_along(block[:, :, width_x - 1 :].astype(jnp.bfloat16), "areal", 1)
    high = passed_along(block[:, :, :1].astype(jnp.bfloat16), "areal", -1)
    west_vals = jnp.concatenate([low.astype(block.dtype), block[:, :, : width_x - 1]], axis=2)
    east_vals = jnp.concatenate([block[:, :, 1:], high.astype(block.dtype)], axis=2)
    return west_vals, east_vals


def shards(
    rhs_base,
    perf_rows,
    perf_cells,
    perf_counts,
    xface_coef,
    xface_dir,
    yface_coef,
    yface_dir,
    cross,
    newton_count,
    sat_diag,
    sat_off,
    col_diag,
    col_off,
):
    f32 = jnp.float32
    slab_depth, comps, width_x, width_y, rhs_count = rhs_base.shape
    layer_count = lax.axis_size("layer")
    tile_count = lax.axis_size("areal")
    depth = slab_depth * layer_count
    part = rhs_count // layer_count

    bf16 = jnp.bfloat16

    def split_bf16(values):
        high = lax.reduce_precision(values, exponent_bits=8, mantissa_bits=7)
        return [high.astype(bf16), (values - high).astype(bf16)]

    def join_bf16(high, low):
        return high.astype(f32) + low.astype(f32)

    is_last = lax.axis_index("areal") == tile_count - 1
    x_local = lax.broadcasted_iota(jnp.int32, xface_coef.shape, 2)
    east_keep = jnp.where(jnp.logical_and(is_last, x_local == width_x - 1), 0.0, 1.0)
    x_signed = xface_coef * (1.0 - 2.0 * xface_dir.astype(f32)) * east_keep
    prev_far = passed_along(jnp.maximum(-x_signed[:, :, width_x - 1], 0.0), "areal", 1)
    y_local = lax.broadcasted_iota(jnp.int32, yface_coef.shape, 3)
    north_keep = jnp.where(y_local == width_y - 1, 0.0, 1.0)
    y_signed = yface_coef * (1.0 - 2.0 * yface_dir.astype(f32)) * north_keep
    identity = jnp.eye(col_off.shape[0], dtype=f32)
    inverse = col_off + identity[:, :, None] * col_diag[:, None, :]
    params = jnp.concatenate([x_signed, y_signed, cross, sat_diag, sat_off], axis=1)
    planes = params.shape[1]

    send_rows = perf_rows.reshape(perf_rows.shape[2:])
    send_cells = perf_cells.reshape(perf_cells.shape[2:])
    send_counts = perf_counts.reshape(perf_counts.shape[2:])
    cap = send_cells.shape[1]
    slot_live = lax.broadcasted_iota(jnp.int32, send_cells.shape, 1) < send_counts[:, None]
    send_rows = jnp.where(slot_live[:, :, None], send_rows, jnp.zeros_like(send_rows))
    cell_code = jnp.concatenate([send_cells // 32, send_cells % 32], axis=1).astype(bf16)
    cell_code = jnp.pad(cell_code, ((0, 0), (0, rhs_count - 2 * cap)))[:, None, :]
    got = lax.all_to_all(
        jnp.concatenate([send_rows, cell_code], axis=1), "areal", split_axis=0, concat_axis=0, tiled=True
    )
    got_rows = got[:, :cap, :]
    got_cells = got[:, cap, :cap].astype(f32) * 32 + got[:, cap, cap : 2 * cap].astype(f32)
    slots = got_cells.size

    lanes = width_y
    rhs_t = jnp.swapaxes(rhs_base, 3, 4).reshape(slab_depth, comps, width_x, layer_count, part, width_y)
    rhs_t = jnp.moveaxis(rhs_t, 3, 0).reshape(layer_count, -1, lanes)
    rows_t = jnp.moveaxis(got_rows.reshape(tile_count, cap, layer_count, part), 2, 0)
    rows_t = rows_t.reshape(layer_count, -1, lanes)
    shared = jnp.concatenate(
        [
            params.reshape(-1, lanes),
            prev_far.reshape(-1, lanes),
            inverse.reshape(-1, lanes),
            got_cells.reshape(-1, lanes),
        ]
    )
    halves = [jnp.broadcast_to(h[None], (layer_count,) + h.shape) for h in split_bf16(shared)]
    payload = jnp.concatenate([rhs_t, rows_t] + halves, axis=1)
    recv = lax.all_to_all(payload, "layer", split_axis=0, concat_axis=0, tiled=True)
    at = rhs_t.shape[1]
    source = recv[:, :at].reshape(depth, comps, width_x, part, width_y).astype(f32)
    size = rows_t.shape[1]
    part_rows = recv[:, at : at + size].reshape(layer_count, slots, part)
    at += size
    size = shared.shape[0]
    shared = join_bf16(recv[:, at : at + size], recv[:, at + size :])
    size = params[0].size // lanes
    params = shared[:, :size].reshape(depth, planes, width_x, width_y)
    prev_far = shared[:, size : size + comps].reshape(depth, comps, 1, width_y)
    at = size + comps
    size = inverse.size // lanes
    inverse = shared[:, at : at + size].reshape(layer_count, depth, depth, -1)
    inverse = jnp.transpose(inverse, (1, 2, 0, 3)).reshape(depth, depth, width_x, 1, width_y)
    all_cells = shared[:, at + size :].reshape(layer_count, slots).astype(jnp.int32)

    tile_cells = slab_depth * width_x * width_y
    one_hot = (
        lax.broadcasted_iota(jnp.int32, (layer_count, slots, tile_cells), 2) == all_cells[:, :, None]
    ).astype(bf16)
    well = jnp.einsum("lsr,lsc->lrc", part_rows, one_hot, preferred_element_type=f32)
    well = well.reshape(layer_count, part, slab_depth, width_x, width_y)
    well = jnp.transpose(well, (0, 2, 3, 1, 4)).reshape(depth, width_x, part, width_y)
    source = source.at[:, 0].add(well)

    x_signed = params[:, 0:3]
    y_signed = params[:, 3:6]
    east_far = jnp.maximum(-x_signed, 0.0)
    north_far = jnp.maximum(-y_signed, 0.0)
    east_w = jnp.maximum(x_signed, 0.0)
    west_w = jnp.concatenate([prev_far, east_far[:, :, : width_x - 1]], axis=2)
    north_w = jnp.maximum(y_signed, 0.0)
    south_w = jnp.concatenate(
        [jnp.zeros_like(north_far[:, :, :, :1]), north_far[:, :, :, : width_y - 1]], axis=3
    )
    east_w, west_w, north_w, south_w = (w[:, :, :, None, :] for w in (east_w, west_w, north_w, south_w))
    params = params[:, :, :, None, :]
    cr = params[:, 6:10]
    sd = params[:, 10:12]
    so = params[:, 12:14]

    step_count = newton_count.shape[0]
    accum_scale = jnp.sum(newton_count).astype(f32) / (step_count * NEWTON_MAX)


    def sweep_rows(center, west_vals, east_vals, rows):
        zero_row = jnp.zeros_like(center[..., :1])
        north_vals = jnp.concatenate([center[..., 1:], zero_row], axis=4)
        south_vals = jnp.concatenate([zero_row, center[..., :-1]], axis=4)
        upwind = (
            east_w[:, :, rows] * (center - east_vals)
            + west_w[:, :, rows] * (west_vals - center)
            + north_w[:, :, rows] * (center - north_vals)
            + south_w[:, :, rows] * (south_vals - center)
        )
        c = cr[:, :, rows]
        mixing = jnp.stack(
            [
                accum_scale * (c[:, 0] * center[:, 1] + c[:, 1] * center[:, 2]),
                accum_scale * c[:, 2] * center[:, 0],
                accum_scale * c[:, 3] * center[:, 0],
            ],
            axis=1,
        )
        balance = source[:, :, rows] - (upwind + mixing)
        return solve(balance, inverse[:, :, rows], sd[:, :, rows], so[:, :, rows])

    def solve(balance, inv, diag, off):
        press_rhs = balance[:, 0]
        new_press = inv[:, 0] * press_rhs[0][None]
        for j in range(1, depth):
            new_press = new_press + inv[:, j] * press_rhs[j][None]
        sat_one = diag[:, 0] * balance[:, 1] + off[:, 0] * balance[:, 2]
        sat_two = off[:, 1] * balance[:, 1] + diag[:, 1] * balance[:, 2]
        return jnp.stack([new_press, sat_one, sat_two], axis=1)

    last_x = width_x - 1
    adjoint = solve(source, inverse, sd, so)
    send_low, send_high = adjoint[:, :, last_x:], adjoint[:, :, :1]
    for sweep_index in range(1, ITERS):
        low = passed_along(send_low.astype(bf16), "areal", 1).astype(f32)
        high = passed_along(send_high.astype(bf16), "areal", -1).astype(f32)
        if sweep_index < ITERS - 1:
            first = sweep_rows(adjoint[:, :, :1], low, adjoint[:, :, 1:2], slice(0, 1))
            last = sweep_rows(
                adjoint[:, :, last_x:], adjoint[:, :, last_x - 1 : last_x], high, slice(last_x, width_x)
            )
            send_low, send_high = last, first
        west_vals = jnp.concatenate([low, adjoint[:, :, :last_x]], axis=2)
        east_vals = jnp.concatenate([adjoint[:, :, 1:], high], axis=2)
        adjoint = sweep_rows(adjoint, west_vals, east_vals, slice(0, width_x))

    out = adjoint.reshape(depth, comps, width_x, 1, part, width_y)
    out = lax.all_to_all(out, "layer", split_axis=0, concat_axis=3, tiled=True)
    out = out.reshape(slab_depth, comps, width_x, rhs_count, width_y)
    return jnp.swapaxes(out, 3, 4)


def solution(mesh):
    in_specs = (
        P("layer", None, "areal", None, None),
        P("areal", "layer", None, None, None),
        P("areal", "layer", None, None),
        P("areal", "layer", None),
        P("layer", None, "areal", None),
        P("layer", None, "areal", None),
        P("layer", None, "areal", None),
        P("layer", None, "areal", None),
        P("layer", None, "areal", None),
        P(),
        P("layer", None, "areal", None),
        P("layer", None, "areal", None),
        P(None, ("areal", "layer")),
        P(None, None, ("areal", "layer")),
    )
    out_specs = P("layer", None, "areal", None, None)
    return jax.shard_map(shards, mesh=mesh, in_specs=in_specs, out_specs=out_specs, check_vma=False)
```

```python
import jax
import jax.numpy as jnp
from jax import lax
from jax.sharding import PartitionSpec as P

ITERS = 4
NEWTON_MAX = 8


def passed_along(block, axis, distance):
    devices = range(lax.axis_size(axis))
    route = [(i - distance, i) for i in devices if i - distance in devices]
    return lax.ppermute(block, axis, route)


def x_neighbours(block):
    width_x = block.shape[2]
    low = passed_along(block[:, :, width_x - 1 :], "areal", 1)
    high = passed_along(block[:, :, :1], "areal", -1)
    west_vals = jnp.concatenate([low, block[:, :, : width_x - 1]], axis=2)
    east_vals = jnp.concatenate([block[:, :, 1:], high], axis=2)
    return west_vals, east_vals


def shards(
    rhs_base,
    perf_rows,
    perf_cells,
    perf_counts,
    xface_coef,
    xface_dir,
    yface_coef,
    yface_dir,
    cross,
    newton_count,
    sat_diag,
    sat_off,
    col_diag,
    col_off,
):
    f32 = jnp.float32
    slab_depth, comps, width_x, width_y, rhs_count = rhs_base.shape
    layer_count = lax.axis_size("layer")
    tile_count = lax.axis_size("areal")
    depth = slab_depth * layer_count
    part = rhs_count // layer_count

    bf16 = jnp.bfloat16

    def split_bf16(values):
        high = lax.reduce_precision(values, exponent_bits=8, mantissa_bits=7)
        return [high.astype(bf16), (values - high).astype(bf16)]

    def join_bf16(high, low):
        return high.astype(f32) + low.astype(f32)

    is_last = lax.axis_index("areal") == tile_count - 1
    x_local = lax.broadcasted_iota(jnp.int32, xface_coef.shape, 2)
    east_keep = jnp.where(jnp.logical_and(is_last, x_local == width_x - 1), 0.0, 1.0)
    x_signed = xface_coef * (1.0 - 2.0 * xface_dir.astype(f32)) * east_keep
    prev_far = passed_along(jnp.maximum(-x_signed[:, :, width_x - 1], 0.0), "areal", 1)
    y_local = lax.broadcasted_iota(jnp.int32, yface_coef.shape, 3)
    north_keep = jnp.where(y_local == width_y - 1, 0.0, 1.0)
    y_signed = yface_coef * (1.0 - 2.0 * yface_dir.astype(f32)) * north_keep
    identity = jnp.eye(col_off.shape[0], dtype=f32)
    inverse = col_off + identity[:, :, None] * col_diag[:, None, :]
    params = jnp.concatenate([x_signed, y_signed, cross, sat_diag, sat_off], axis=1)
    planes = params.shape[1]

    send_rows = perf_rows.reshape(perf_rows.shape[2:])
    send_cells = perf_cells.reshape(perf_cells.shape[2:])
    send_counts = perf_counts.reshape(perf_counts.shape[2:])
    cap = send_cells.shape[1]
    slot_live = lax.broadcasted_iota(jnp.int32, send_cells.shape, 1) < send_counts[:, None]
    send_rows = jnp.where(slot_live[:, :, None], send_rows, jnp.zeros_like(send_rows))
    cell_code = jnp.concatenate([send_cells // 32, send_cells % 32], axis=1).astype(bf16)
    cell_code = jnp.pad(cell_code, ((0, 0), (0, rhs_count - 2 * cap)))[:, None, :]
    got = lax.all_to_all(
        jnp.concatenate([send_rows, cell_code], axis=1), "areal", split_axis=0, concat_axis=0, tiled=True
    )
    got_rows = got[:, :cap, :]
    got_cells = got[:, cap, :cap].astype(f32) * 32 + got[:, cap, cap : 2 * cap].astype(f32)
    slots = got_cells.size

    lanes = width_y
    rhs_t = jnp.swapaxes(rhs_base, 3, 4).reshape(slab_depth, comps, width_x, layer_count, part, width_y)
    rhs_t = jnp.moveaxis(rhs_t, 3, 0).reshape(layer_count, -1, lanes)
    rows_t = jnp.moveaxis(got_rows.reshape(tile_count, cap, layer_count, part), 2, 0)
    rows_t = rows_t.reshape(layer_count, -1, lanes)
    shared = jnp.concatenate(
        [
            params.reshape(-1, lanes),
            prev_far.reshape(-1, lanes),
            inverse.reshape(-1, lanes),
            got_cells.reshape(-1, lanes),
        ]
    )
    halves = [jnp.broadcast_to(h[None], (layer_count,) + h.shape) for h in split_bf16(shared)]
    payload = jnp.concatenate([rhs_t, rows_t] + halves, axis=1)
    recv = lax.all_to_all(payload, "layer", split_axis=0, concat_axis=0, tiled=True)
    at = rhs_t.shape[1]
    source = recv[:, :at].reshape(depth, comps, width_x, part, width_y).astype(f32)
    size = rows_t.shape[1]
    part_rows = recv[:, at : at + size].reshape(layer_count, slots, part)
    at += size
    size = shared.shape[0]
    shared = join_bf16(recv[:, at : at + size], recv[:, at + size :])
    size = params[0].size // lanes
    params = shared[:, :size].reshape(depth, planes, width_x, width_y)
    prev_far = shared[:, size : size + comps].reshape(depth, comps, 1, width_y)
    at = size + comps
    size = inverse.size // lanes
    inverse = shared[:, at : at + size].reshape(layer_count, depth, depth, -1)
    inverse = jnp.transpose(inverse, (1, 2, 0, 3)).reshape(depth, depth, width_x, 1, width_y)
    all_cells = shared[:, at + size :].reshape(layer_count, slots).astype(jnp.int32)

    tile_cells = slab_depth * width_x * width_y
    one_hot = (
        lax.broadcasted_iota(jnp.int32, (layer_count, slots, tile_cells), 2) == all_cells[:, :, None]
    ).astype(bf16)
    well = jnp.einsum("lsr,lsc->lrc", part_rows, one_hot, preferred_element_type=f32)
    well = well.reshape(layer_count, part, slab_depth, width_x, width_y)
    well = jnp.transpose(well, (0, 2, 3, 1, 4)).reshape(depth, width_x, part, width_y)
    source = source.at[:, 0].add(well)

    x_signed = params[:, 0:3]
    y_signed = params[:, 3:6]
    east_far = jnp.maximum(-x_signed, 0.0)
    north_far = jnp.maximum(-y_signed, 0.0)
    east_w = jnp.maximum(x_signed, 0.0)
    west_w = jnp.concatenate([prev_far, east_far[:, :, : width_x - 1]], axis=2)
    north_w = jnp.maximum(y_signed, 0.0)
    south_w = jnp.concatenate(
        [jnp.zeros_like(north_far[:, :, :, :1]), north_far[:, :, :, : width_y - 1]], axis=3
    )
    east_w, west_w, north_w, south_w = (w[:, :, :, None, :] for w in (east_w, west_w, north_w, south_w))
    params = params[:, :, :, None, :]
    cr = params[:, 6:10]
    sd = params[:, 10:12]
    so = params[:, 12:14]

    step_count = newton_count.shape[0]
    accum_scale = jnp.sum(newton_count).astype(f32) / (step_count * NEWTON_MAX)


    adjoint = None
    for sweep_index in range(ITERS):
        if sweep_index == 0:
            balance = source
        else:
            west_vals, east_vals = x_neighbours(adjoint)
            zero_row = jnp.zeros_like(adjoint[..., :1])
            north_vals = jnp.concatenate([adjoint[..., 1:], zero_row], axis=4)
            south_vals = jnp.concatenate([zero_row, adjoint[..., :-1]], axis=4)
            upwind = (
                east_w * (adjoint - east_vals)
                + west_w * (west_vals - adjoint)
                + north_w * (adjoint - north_vals)
                + south_w * (south_vals - adjoint)
            )
            mixing = jnp.stack(
                [
                    accum_scale * (cr[:, 0] * adjoint[:, 1] + cr[:, 1] * adjoint[:, 2]),
                    accum_scale * cr[:, 2] * adjoint[:, 0],
                    accum_scale * cr[:, 3] * adjoint[:, 0],
                ],
                axis=1,
            )
            balance = source - (upwind + mixing)
        press_rhs = balance[:, 0]
        new_press = inverse[:, 0] * press_rhs[0][None]
        for j in range(1, depth):
            new_press = new_press + inverse[:, j] * press_rhs[j][None]
        sat_one = sd[:, 0] * balance[:, 1] + so[:, 0] * balance[:, 2]
        sat_two = so[:, 1] * balance[:, 1] + sd[:, 1] * balance[:, 2]
        adjoint = jnp.stack([new_press, sat_one, sat_two], axis=1)

    out = adjoint.reshape(depth, comps, width_x, 1, part, width_y)
    out = lax.all_to_all(out, "layer", split_axis=0, concat_axis=3, tiled=True)
    out = out.reshape(slab_depth, comps, width_x, rhs_count, width_y)
    return jnp.swapaxes(out, 3, 4)


def solution(mesh):
    in_specs = (
        P("layer", None, "areal", None, None),
        P("areal", "layer", None, None, None),
        P("areal", "layer", None, None),
        P("areal", "layer", None),
        P("layer", None, "areal", None),
        P("layer", None, "areal", None),
        P("layer", None, "areal", None),
        P("layer", None, "areal", None),
        P("layer", None, "areal", None),
        P(),
        P("layer", None, "areal", None),
        P("layer", None, "areal", None),
        P(None, ("areal", "layer")),
        P(None, None, ("areal", "layer")),
    )
    out_specs = P("layer", None, "areal", None, None)
    return jax.shard_map(shards, mesh=mesh, in_specs=in_specs, out_specs=out_specs, check_vma=False)
```

```python
import jax
import jax.numpy as jnp
from jax import lax
from jax.sharding import PartitionSpec as P

ITERS = 4
NEWTON_MAX = 8


def passed_along(block, axis, distance):
    devices = range(lax.axis_size(axis))
    route = [(i - distance, i) for i in devices if i - distance in devices]
    return lax.ppermute(block, axis, route)


def x_neighbours(block):
    width_x = block.shape[2]
    low = passed_along(block[:, :, width_x - 1 :].astype(jnp.bfloat16), "areal", 1)
    high = passed_along(block[:, :, :1].astype(jnp.bfloat16), "areal", -1)
    west_vals = jnp.concatenate([low.astype(block.dtype), block[:, :, : width_x - 1]], axis=2)
    east_vals = jnp.concatenate([block[:, :, 1:], high.astype(block.dtype)], axis=2)
    return west_vals, east_vals


def shards(
    rhs_base,
    perf_rows,
    perf_cells,
    perf_counts,
    xface_coef,
    xface_dir,
    yface_coef,
    yface_dir,
    cross,
    newton_count,
    sat_diag,
    sat_off,
    col_diag,
    col_off,
):
    f32 = jnp.float32
    slab_depth, comps, width_x, width_y, rhs_count = rhs_base.shape
    layer_count = lax.axis_size("layer")
    tile_count = lax.axis_size("areal")
    depth = slab_depth * layer_count
    part = rhs_count // layer_count

    bf16 = jnp.bfloat16

    def split_bf16(values):
        high = lax.reduce_precision(values, exponent_bits=8, mantissa_bits=7)
        return [high.astype(bf16), (values - high).astype(bf16)]

    def join_bf16(high, low):
        return high.astype(f32) + low.astype(f32)

    is_last = lax.axis_index("areal") == tile_count - 1
    x_local = lax.broadcasted_iota(jnp.int32, xface_coef.shape, 2)
    east_keep = jnp.where(jnp.logical_and(is_last, x_local == width_x - 1), 0.0, 1.0)
    x_signed = xface_coef * (1.0 - 2.0 * xface_dir.astype(f32)) * east_keep
    prev_far = passed_along(jnp.maximum(-x_signed[:, :, width_x - 1], 0.0), "areal", 1)
    y_local = lax.broadcasted_iota(jnp.int32, yface_coef.shape, 3)
    north_keep = jnp.where(y_local == width_y - 1, 0.0, 1.0)
    y_signed = yface_coef * (1.0 - 2.0 * yface_dir.astype(f32)) * north_keep
    identity = jnp.eye(col_off.shape[0], dtype=f32)
    inverse = col_off + identity[:, :, None] * col_diag[:, None, :]
    params = jnp.concatenate([x_signed, y_signed, cross, sat_diag, sat_off], axis=1)
    planes = params.shape[1]

    send_rows = perf_rows.reshape(perf_rows.shape[2:])
    send_cells = perf_cells.reshape(perf_cells.shape[2:])
    send_counts = perf_counts.reshape(perf_counts.shape[2:])
    cap = send_cells.shape[1]
    slot_live = lax.broadcasted_iota(jnp.int32, send_cells.shape, 1) < send_counts[:, None]
    tile_cells = slab_depth * width_x * width_y
    send_cells = jnp.where(slot_live, send_cells, send_cells + tile_cells)
    cell_code = jnp.concatenate([send_cells // 32, send_cells % 32], axis=1).astype(bf16)
    cell_code = jnp.pad(cell_code, ((0, 0), (0, rhs_count - 2 * cap)))[:, None, :]
    got = lax.all_to_all(
        jnp.concatenate([send_rows, cell_code], axis=1), "areal", split_axis=0, concat_axis=0, tiled=True
    )
    got_rows = got[:, :cap, :]
    got_cells = got[:, cap, :cap].astype(f32) * 32 + got[:, cap, cap : 2 * cap].astype(f32)
    slots = got_cells.size

    lanes = width_y
    rhs_t = jnp.swapaxes(rhs_base, 3, 4).reshape(slab_depth, comps, width_x, layer_count, part, width_y)
    rhs_t = jnp.moveaxis(rhs_t, 3, 0).reshape(layer_count, -1, lanes)
    rows_t = jnp.moveaxis(got_rows.reshape(tile_count, cap, layer_count, part), 2, 0)
    rows_t = rows_t.reshape(layer_count, -1, lanes)
    shared = jnp.concatenate(
        [
            params.reshape(-1, lanes),
            prev_far.reshape(-1, lanes),
            inverse.reshape(-1, lanes),
            got_cells.reshape(-1, lanes),
        ]
    )
    halves = [jnp.broadcast_to(h[None], (layer_count,) + h.shape) for h in split_bf16(shared)]
    payload = jnp.concatenate([rhs_t, rows_t] + halves, axis=1)
    recv = lax.all_to_all(payload, "layer", split_axis=0, concat_axis=0, tiled=True)
    at = rhs_t.shape[1]
    source = recv[:, :at].reshape(depth, comps, width_x, part, width_y).astype(f32)
    size = rows_t.shape[1]
    part_rows = recv[:, at : at + size].reshape(layer_count, slots, part)
    at += size
    size = shared.shape[0]
    shared = join_bf16(recv[:, at : at + size], recv[:, at + size :])
    size = params[0].size // lanes
    params = shared[:, :size].reshape(depth, planes, width_x, width_y)
    prev_far = shared[:, size : size + comps].reshape(depth, comps, 1, width_y)
    at = size + comps
    size = inverse.size // lanes
    inverse = shared[:, at : at + size].reshape(layer_count, depth, depth, -1)
    inverse = jnp.transpose(inverse, (1, 2, 0, 3)).reshape(depth, depth, width_x, 1, width_y)
    all_cells = shared[:, at + size :].reshape(layer_count, slots).astype(jnp.int32)

    tile_cells = slab_depth * width_x * width_y
    one_hot = (
        lax.broadcasted_iota(jnp.int32, (layer_count, slots, tile_cells), 2) == all_cells[:, :, None]
    ).astype(bf16)
    well = jnp.einsum("lsr,lsc->lrc", part_rows, one_hot, preferred_element_type=f32)
    well = well.reshape(layer_count, part, slab_depth, width_x, width_y)
    well = jnp.transpose(well, (0, 2, 3, 1, 4)).reshape(depth, width_x, part, width_y)
    source = source.at[:, 0].add(well)

    x_signed = params[:, 0:3]
    y_signed = params[:, 3:6]
    east_far = jnp.maximum(-x_signed, 0.0)
    north_far = jnp.maximum(-y_signed, 0.0)
    east_w = jnp.maximum(x_signed, 0.0)
    west_w = jnp.concatenate([prev_far, east_far[:, :, : width_x - 1]], axis=2)
    north_w = jnp.maximum(y_signed, 0.0)
    south_w = jnp.concatenate(
        [jnp.zeros_like(north_far[:, :, :, :1]), north_far[:, :, :, : width_y - 1]], axis=3
    )
    east_w, west_w, north_w, south_w = (w[:, :, :, None, :] for w in (east_w, west_w, north_w, south_w))
    params = params[:, :, :, None, :]
    cr = params[:, 6:10]
    sd = params[:, 10:12]
    so = params[:, 12:14]

    step_count = newton_count.shape[0]
    accum_scale = jnp.sum(newton_count).astype(f32) / (step_count * NEWTON_MAX)


    adjoint = None
    for sweep_index in range(ITERS):
        if sweep_index == 0:
            balance = source
        else:
            west_vals, east_vals = x_neighbours(adjoint)
            zero_row = jnp.zeros_like(adjoint[..., :1])
            north_vals = jnp.concatenate([adjoint[..., 1:], zero_row], axis=4)
            south_vals = jnp.concatenate([zero_row, adjoint[..., :-1]], axis=4)
            upwind = (
                east_w * (adjoint - east_vals)
                + west_w * (west_vals - adjoint)
                + north_w * (adjoint - north_vals)
                + south_w * (south_vals - adjoint)
            )
            mixing = jnp.stack(
                [
                    accum_scale * (cr[:, 0] * adjoint[:, 1] + cr[:, 1] * adjoint[:, 2]),
                    accum_scale * cr[:, 2] * adjoint[:, 0],
                    accum_scale * cr[:, 3] * adjoint[:, 0],
                ],
                axis=1,
            )
            balance = source - (upwind + mixing)
        press_rhs = balance[:, 0]
        new_press = inverse[:, 0] * press_rhs[0][None]
        for j in range(1, depth):
            new_press = new_press + inverse[:, j] * press_rhs[j][None]
        sat_one = sd[:, 0] * balance[:, 1] + so[:, 0] * balance[:, 2]
        sat_two = so[:, 1] * balance[:, 1] + sd[:, 1] * balance[:, 2]
        adjoint = jnp.stack([new_press, sat_one, sat_two], axis=1)

    out = adjoint.reshape(depth, comps, width_x, 1, part, width_y)
    out = lax.all_to_all(out, "layer", split_axis=0, concat_axis=3, tiled=True)
    out = out.reshape(slab_depth, comps, width_x, rhs_count, width_y)
    return jnp.swapaxes(out, 3, 4)


def solution(mesh):
    in_specs = (
        P("layer", None, "areal", None, None),
        P("areal", "layer", None, None, None),
        P("areal", "layer", None, None),
        P("areal", "layer", None),
        P("layer", None, "areal", None),
        P("layer", None, "areal", None),
        P("layer", None, "areal", None),
        P("layer", None, "areal", None),
        P("layer", None, "areal", None),
        P(),
        P("layer", None, "areal", None),
        P("layer", None, "areal", None),
        P(None, ("areal", "layer")),
        P(None, None, ("areal", "layer")),
    )
    out_specs = P("layer", None, "areal", None, None)
    return jax.shard_map(shards, mesh=mesh, in_specs=in_specs, out_specs=out_specs, check_vma=False)
```
